128 devices in a mesh: pipe: 4 (over x), expert: 32 (over z, y, core).
Axes of the slice: x: 4, y: 4, z: 4, core: 2. Of those that a mesh axis runs over, the one named last changes fastest.
Arguments:
- out_grad: bfloat16 [4, 4096, 2560], P('pipe', 'expert'), may hold values from -1.5 to 1.5
- layer_input: bfloat16 [4, 4096, 2560], P('pipe', 'expert'), may hold values from -6 to 6
- route_ids: int32 [4, 4096, 6], P('pipe', 'expert'), may hold values from 0 to 31, all different within a row; in each aligned block of 128 rows (0 to 127, 128 to 255, ..., all dimensions but the last counted through in order) at most 28 rows name the same one
- route_probs: float32 [4, 4096, 6], P('pipe', 'expert'), may hold values from 0.03 to 0.5
- gate_weight: bfloat16 [4, 32, 2560, 768], P('pipe', 'expert'), may hold values from -0.125 to 0.125
- up_weight: bfloat16 [4, 32, 2560, 768], P('pipe', 'expert'), may hold values from -0.125 to 0.125
- down_weight: bfloat16 [4, 32, 768, 2560], P('pipe', 'expert'), may hold values from -0.21875 to 0.21875
Outputs:
- prev_grad: bfloat16 [4, 4096, 2560], P('pipe', 'expert')
- gate_grad: bfloat16 [4, 4096, 6], P('pipe', 'expert')
The draws below stay inside these ranges and needn't reach their ends.
Inputs may be any that keep to these rules, and one draw needn't show every extreme that they name: `route_ids`: each token names 6 different experts; the 128 tokens of one aligned block name one expert at most 28 times, and some block reaches 28.
All inputs are finite; a program needn't handle non-finite values.
Results may differ from the reference program's by a relative error of at most 0.004.
Values may be sent and summed in bfloat16 or wider, within the bound.
No kernel may reach another device: no remote copies, remote signals or barrier semaphores. Data moves between devices by JAX's collectives and lax.ppermute only.
A program may use at most 128 MiB of HBM per device.

```python
import math
import jax
import jax.numpy as jnp
import numpy as np
from jax import lax

D = 2560
F = 768
TOPK = 6
TOK_DEV = 128
SECTIONS = 4
EXPERTS = 32
TOKENS = 4096
CAP = 28
N_EXPERT = 32


def steps_of(rng, extent, shards, smallest, largest):
    factor_of = 1.0
    for axis_at, parts in shards:
        heights = jax.random.uniform(jax.random.fold_in(jax.random.fold_in(rng, 6), axis_at), (parts,), jnp.float32, smallest / len(shards), largest / len(shards))
        factor_of = factor_of * jnp.repeat(jnp.exp(heights), extent[axis_at] // parts).reshape((-1,) + (1,) * (len(extent) - 1 - axis_at))
    return factor_of


def assign_block(own_key, own, number, rows, count, top, bound, skew):
    ranking = jax.random.permutation(own_key, count)
    packed, ordinary = shares(count, rows * top, bound, skew, True), shares(count, rows * top, bound, skew, False)
    places = jnp.arange(count)

    def named(sizes, offset_by):
        used = int((sizes > 0).sum())
        fixed = max(1, used // 4)
        shifted = fixed + (places - fixed + offset_by * (used - fixed)) % max(1, count - fixed)
        return jnp.zeros((count,), jnp.int32).at[ranking[jnp.where(places < fixed, places, shifted)]].set(jnp.asarray(sizes, jnp.int32))

    sizes = jnp.where(number % 4 == 0, named(packed, number // 4), named(ordinary, number - number // 4 - 1))
    mixed = jax.random.permutation(jax.random.fold_in(own, 3), count)
    source_of, receiver = mixed[0:count // 2 * 2:2], mixed[1:count // 2 * 2:2]
    room = jnp.minimum(sizes[source_of] - 1, bound - sizes[receiver]) // 2
    room = jnp.where((source_of == ranking[0]) | (receiver == ranking[0]) | (sizes[receiver] == 0), 0, jnp.maximum(room, 0))
    shifted = jax.random.randint(jax.random.fold_in(own, 4), (count // 2,), 0, 1 << 20) % (room + 1)
    sizes = sizes.at[source_of].add(-shifted).at[receiver].add(shifted)
    members = jnp.searchsorted(jnp.cumsum(sizes), jnp.arange(rows * top), side="right").astype(jnp.int32)
    table = members.reshape(top, rows).T
    table = table[jax.random.permutation(jax.random.fold_in(own, 1), rows)]
    offset_by = jax.random.randint(jax.random.fold_in(own, 2), (rows, 1), 0, top)
    return jnp.take_along_axis(table, (jnp.arange(top)[None, :] + offset_by) % top, axis=1)


def shares(number_of, total, reach, lean, full):
    portions = [(1 << 20) // math.isqrt(standing ** lean) + 1 for standing in range(1, number_of + 1)]
    largest = reach if full else min(reach, max(-(-total // number_of), total * portions[0] // sum(portions)))
    least = 1 if total - largest >= number_of - 1 else 0
    counts, rest = [largest] + [least] * (number_of - 1), total - largest - least * (number_of - 1)
    while rest > 0:
        movable = [i for i in range(1, number_of) if counts[i] < largest] or [i for i in range(1, number_of) if counts[i] < reach]
        whole, left = sum([portions[i] for i in movable]), rest
        for i in movable:
            addition = min(reach - counts[i], max(1, left * portions[i] // whole), rest)
            counts[i] = counts[i] + addition
            rest = rest - addition
    return np.array(counts)


def centred(rng, extent, scale, bound, split=(), kind=jnp.bfloat16):
    array = jax.random.normal(rng, extent, jnp.float32) * scale
    if len(split) > 0:
        array = steps_of(rng, extent, split, -0.22, 0.18) * array
    return jnp.clip(array, min=-bound, max=bound).astype(kind)


def setup_inputs(seed: int = 0) -> dict:
    splits = jax.random.split(jax.random.key(seed), 8)
    out_grad = centred(splits[0], (SECTIONS, TOKENS, D), 0.25, 1.5, ((0, 4), (1, 32)))
    layer_input = centred(splits[1], (SECTIONS, TOKENS, D), 1.0, 6.0, ((0, 4), (1, 32)))
    route_ids_keys = jax.random.split(jax.random.fold_in(splits[2], 1), SECTIONS * TOKENS // TOK_DEV)
    route_ids_turns = jax.random.permutation(jax.random.fold_in(splits[2], 3), SECTIONS * TOKENS // TOK_DEV)
    route_ids = jax.vmap(lambda own, number: assign_block(jax.random.fold_in(splits[2], 2), own, number, TOK_DEV, EXPERTS, TOPK, CAP, 1))(route_ids_keys, route_ids_turns).reshape((SECTIONS, TOKENS, TOPK))
    route_probs = jnp.clip(jnp.exp(math.log(0.5) - 2.8134107 * jax.random.uniform(splits[3], (SECTIONS, TOKENS, TOPK), jnp.float32) ** steps_of(splits[3], (SECTIONS, TOKENS, TOPK), ((0, 4), (1, 32)), -0.2, 0.2)), 0.03, 0.5)
    gate_weight = centred(splits[4], (SECTIONS, EXPERTS, D, F), D ** -0.5, 0.125, ((0, 4), (1, 32)))
    up_weight = centred(splits[5], (SECTIONS, EXPERTS, D, F), D ** -0.5, 0.125, ((0, 4), (1, 32)))
    down_weight = centred(splits[6], (SECTIONS, EXPERTS, F, D), F ** -0.5, 0.21875, ((0, 4), (1, 32)))
    return {"out_grad": out_grad, "layer_input": layer_input, "route_ids": route_ids, "route_probs": route_probs, "gate_weight": gate_weight, "up_weight": up_weight, "down_weight": down_weight}


def expert_rows(grad_rows, input_rows, gate_matrix, up_matrix, down_matrix):
    gate_pre = jnp.dot(input_rows, gate_matrix, preferred_element_type=jnp.float32)
    up_pre = jnp.dot(input_rows, up_matrix, preferred_element_type=jnp.float32)
    hidden_grad = jnp.dot(grad_rows, down_matrix.T, preferred_element_type=jnp.float32)
    sigmoid = jax.nn.sigmoid(gate_pre)
    active = gate_pre * sigmoid
    gate_value = jnp.sum(hidden_grad * active * up_pre, axis=-1).astype(jnp.bfloat16)
    gate_back = (hidden_grad * up_pre * sigmoid * (1.0 + gate_pre * (1.0 - sigmoid))).astype(jnp.bfloat16)
    up_back = (hidden_grad * active).astype(jnp.bfloat16)
    input_back = jnp.dot(gate_back, gate_matrix.T, preferred_element_type=jnp.float32) + jnp.dot(up_back, up_matrix.T, preferred_element_type=jnp.float32)
    return input_back.astype(jnp.bfloat16), gate_value


def section_pass(section_args):
    grad_tokens, input_tokens, chosen, slot_probs, gate_all, up_all, down_all = section_args
    block_ids = chosen.reshape(N_EXPERT, TOK_DEV * TOPK)
    one_hot = (block_ids[:, :, None] == jnp.arange(EXPERTS, dtype=jnp.int32)[None, None, :]).astype(jnp.int32)
    places = jnp.sum(one_hot * jnp.cumsum(one_hot, axis=1), axis=2) - 1
    target = (block_ids * CAP + places).astype(jnp.int32)
    block_rows = jnp.arange(N_EXPERT, dtype=jnp.int32)[:, None]
    values = jnp.broadcast_to(jnp.arange(TOK_DEV * TOPK, dtype=jnp.int32)[None, :], target.shape)
    slot_table = jnp.full((N_EXPERT, EXPERTS * CAP), -1, jnp.int32).at[block_rows, target].set(values)
    slot_table = slot_table.reshape(N_EXPERT, EXPERTS, CAP).transpose(1, 0, 2).reshape(EXPERTS, N_EXPERT * CAP)
    block_index = jnp.repeat(jnp.arange(N_EXPERT, dtype=jnp.int32), CAP)

    def per_expert(carry, inputs):
        running, gate_sum = carry
        slots, gate_matrix, up_matrix, down_matrix = inputs
        filled = slots >= 0
        local_slot = jnp.where(filled, slots, 0)
        token_index = (block_index * TOK_DEV + local_slot // TOPK).astype(jnp.int32)
        slot_index = (local_slot % TOPK).astype(jnp.int32)
        zero_value = jnp.zeros((), grad_tokens.dtype)
        grad_rows = jnp.where(filled[:, None], grad_tokens[token_index], zero_value)
        input_rows = jnp.where(filled[:, None], input_tokens[token_index], zero_value)
        input_back, gate_value = expert_rows(grad_rows, input_rows, gate_matrix, up_matrix, down_matrix)
        weight = jnp.where(filled, slot_probs[token_index, slot_index], jnp.zeros((), slot_probs.dtype))
        running = running.at[token_index].add(weight[:, None] * input_back.astype(slot_probs.dtype))
        gate_sum = gate_sum.at[token_index, slot_index].add(jnp.where(filled, gate_value.astype(slot_probs.dtype), jnp.zeros((), slot_probs.dtype)))
        return (running, gate_sum), None

    start = (grad_tokens.astype(jnp.float32), jnp.zeros((TOKENS, TOPK), jnp.float32))
    (running, gate_sum), unused = lax.scan(per_expert, start, (slot_table, gate_all, up_all, down_all))
    return running.astype(jnp.bfloat16), gate_sum.astype(jnp.bfloat16)


def reference(out_grad, layer_input, route_ids, route_probs, gate_weight, up_weight, down_weight):
    input_grad, gate_grad = lax.map(section_pass, (out_grad, layer_input, route_ids, route_probs, gate_weight, up_weight, down_weight))
    prev_grad = jnp.concatenate([input_grad[1:], jnp.zeros_like(input_grad[:1])], axis=0)
    return prev_grad, gate_grad
```

```python
import jax
import jax.numpy as jnp
from jax import lax
from jax.sharding import PartitionSpec as P


def passed_along(value, axis, steps):
    count = lax.axis_size(axis)
    first, last = (max(0, -steps), min(count, count - steps))
    return lax.ppermute(value, axis, [(source, source + steps) for source in range(first, last)])


def expert_rows(grad_rows, input_rows, gate_matrix, up_matrix, down_matrix):
    gate_pre = jnp.dot(input_rows, gate_matrix, preferred_element_type=jnp.float32)
    up_pre = jnp.dot(input_rows, up_matrix, preferred_element_type=jnp.float32)
    hidden_grad = lax.dot_general(
        grad_rows, down_matrix, (((1,), (1,)), ((), ())), preferred_element_type=jnp.float32
    )
    sigmoid = jax.nn.sigmoid(gate_pre)
    active = gate_pre * sigmoid
    gate_value = jnp.sum(hidden_grad * active * up_pre, axis=-1).astype(jnp.bfloat16)
    gate_part = (hidden_grad * up_pre * sigmoid * (1.0 + gate_pre * (1.0 - sigmoid))).astype(
        jnp.bfloat16
    )
    up_part = (hidden_grad * active).astype(jnp.bfloat16)
    input_back = lax.dot_general(
        gate_part, gate_matrix, (((1,), (1,)), ((), ())), preferred_element_type=jnp.float32
    ) + lax.dot_general(
        up_part, up_matrix, (((1,), (1,)), ((), ())), preferred_element_type=jnp.float32
    )
    return input_back.astype(jnp.bfloat16), gate_value


def body(out_grad, layer_input, route_ids, route_probs, gate_weight, up_weight, down_weight):
    grad_tokens = out_grad[0]
    input_tokens = layer_input[0]
    chosen = route_ids[0]
    slot_probs = route_probs[0]
    gate_matrix = gate_weight[0, 0]
    up_matrix = up_weight[0, 0]
    down_matrix = down_weight[0, 0]
    peer_count = lax.axis_size("expert")
    token_count, top_count = chosen.shape
    model_width = grad_tokens.shape[1]
    capacity = min(token_count, 7 * token_count * top_count // (6 * peer_count))
    rows = peer_count * capacity

    flat_ids = chosen.reshape(-1)
    one_hot = (flat_ids[:, None] == jnp.arange(peer_count, dtype=jnp.int32)[None, :]).astype(
        jnp.int32
    )
    places = jnp.sum(one_hot * jnp.cumsum(one_hot, axis=0), axis=1) - 1
    target = (flat_ids * capacity + places).reshape(token_count, top_count)

    hits = target[:, :, None] == jnp.arange(rows, dtype=jnp.int32)[None, None, :]
    pick = jnp.any(hits, axis=1).astype(jnp.bfloat16)
    both = jnp.concatenate([grad_tokens, input_tokens], axis=1)
    send = lax.dot_general(
        pick, both, (((0,), (0,)), ((), ())), preferred_element_type=jnp.float32
    ).astype(jnp.bfloat16)
    send = send.reshape(peer_count, capacity, 2 * model_width)
    arrived = lax.all_to_all(send, "expert", 0, 0, tiled=True)
    arrived = arrived.reshape(rows, 2 * model_width)
    back, gate_value = expert_rows(
        arrived[:, :model_width], arrived[:, model_width:], gate_matrix, up_matrix, down_matrix
    )
    returned = lax.all_to_all(
        back.reshape(peer_count, capacity, model_width), "expert", 0, 0, tiled=True
    ).reshape(rows, model_width)
    gate_back = lax.all_to_all(
        gate_value.reshape(peer_count, capacity), "expert", 0, 0, tiled=True
    ).reshape(rows)

    weights = jnp.sum(jnp.where(hits, slot_probs[:, :, None], 0.0), axis=1)
    combined = grad_tokens.astype(jnp.float32) + jnp.dot(
        weights,
        returned.astype(jnp.float32),
        precision=lax.Precision.HIGHEST,
        preferred_element_type=jnp.float32,
    )
    gate_slot = gate_back[target.reshape(-1)].reshape(token_count, top_count)
    passed = passed_along(combined.astype(jnp.bfloat16), "pipe", -1)
    return (passed[None], gate_slot[None])


def solution(mesh):
    placed = (
        P("pipe", "expert", None),
        P("pipe", "expert", None),
        P("pipe", "expert", None),
        P("pipe", "expert", None),
        P("pipe", "expert", None, None),
        P("pipe", "expert", None, None),
        P("pipe", "expert", None, None),
    )
    return jax.shard_map(
        body,
        mesh=mesh,
        in_specs=placed,
        out_specs=(P("pipe", "expert", None), P("pipe", "expert", None)),
        check_vma=False,
    )
```

```python
import jax
import jax.numpy as jnp
from jax import lax
from jax.sharding import PartitionSpec as P


def passed_along(value, axis, steps):
    count = lax.axis_size(axis)
    first, last = (max(0, -steps), min(count, count - steps))
    return lax.ppermute(value, axis, [(source, source + steps) for source in range(first, last)])


def expert_rows(grad_rows, input_rows, gate_matrix, up_matrix, down_matrix):
    gate_pre = jnp.dot(input_rows, gate_matrix, preferred_element_type=jnp.float32)
    up_pre = jnp.dot(input_rows, up_matrix, preferred_element_type=jnp.float32)
    hidden_grad = lax.dot_general(
        grad_rows, down_matrix, (((1,), (1,)), ((), ())), preferred_element_type=jnp.float32
    )
    sigmoid = jax.nn.sigmoid(gate_pre)
    active = gate_pre * sigmoid
    gate_value = jnp.sum(hidden_grad * active * up_pre, axis=-1).astype(jnp.bfloat16)
    gate_part = (hidden_grad * up_pre * sigmoid * (1.0 + gate_pre * (1.0 - sigmoid))).astype(
        jnp.bfloat16
    )
    up_part = (hidden_grad * active).astype(jnp.bfloat16)
    input_back = lax.dot_general(
        gate_part, gate_matrix, (((1,), (1,)), ((), ())), preferred_element_type=jnp.float32
    ) + lax.dot_general(
        up_part, up_matrix, (((1,), (1,)), ((), ())), preferred_element_type=jnp.float32
    )
    return input_back.astype(jnp.bfloat16), gate_value


def body(out_grad, layer_input, route_ids, route_probs, gate_weight, up_weight, down_weight):
    grad_tokens = out_grad[0]
    input_tokens = layer_input[0]
    chosen = route_ids[0]
    slot_probs = route_probs[0]
    gate_matrix = gate_weight[0, 0]
    up_matrix = up_weight[0, 0]
    down_matrix = down_weight[0, 0]
    peer_count = lax.axis_size("expert")
    token_count, top_count = chosen.shape
    model_width = grad_tokens.shape[1]
    capacity = min(token_count, 7 * token_count * top_count // (6 * peer_count))
    chunk = -(-(capacity + 1) // 16) * 8
    rows = peer_count * chunk

    flat_ids = chosen.reshape(-1)
    one_hot = (flat_ids[:, None] == jnp.arange(peer_count, dtype=jnp.int32)[None, :]).astype(
        jnp.int32
    )
    places = (jnp.sum(one_hot * jnp.cumsum(one_hot, axis=0), axis=1) - 1).reshape(
        token_count, top_count
    )
    ids = chosen
    lanes = jnp.arange(rows, dtype=jnp.int32)[None, None, :]
    both = jnp.concatenate([grad_tokens, input_tokens], axis=1)
    gate_row = chunk - 1

    def dispatch(part):
        local = places - part * chunk
        inside = (local >= 0) & (local < chunk)
        target = jnp.where(inside, ids * chunk + local, -1)
        hits = target[:, :, None] == lanes
        pick = jnp.any(hits, axis=1).astype(jnp.bfloat16)
        send = lax.dot_general(
            pick, both, (((0,), (0,)), ((), ())), preferred_element_type=jnp.float32
        ).astype(jnp.bfloat16)
        weights = jnp.sum(jnp.where(hits, slot_probs[:, :, None], 0.0), axis=1)
        return send.reshape(peer_count, chunk, 2 * model_width), weights

    send_a, weights_a = dispatch(0)
    send_b, weights_b = dispatch(1)
    arrived_a = lax.all_to_all(send_a, "expert", 0, 0, tiled=True).reshape(rows, 2 * model_width)
    arrived_b = lax.all_to_all(send_b, "expert", 0, 0, tiled=True).reshape(rows, 2 * model_width)
    back_a, gate_a = expert_rows(
        arrived_a[:, :model_width], arrived_a[:, model_width:], gate_matrix, up_matrix, down_matrix
    )
    returned_a = lax.all_to_all(
        back_a.reshape(peer_count, chunk, model_width), "expert", 0, 0, tiled=True
    ).reshape(rows, model_width)
    back_b, gate_b = expert_rows(
        arrived_b[:, :model_width], arrived_b[:, model_width:], gate_matrix, up_matrix, down_matrix
    )
    gates = jnp.concatenate(
        [gate_a.reshape(peer_count, chunk), gate_b.reshape(peer_count, chunk)], axis=1
    )
    gates = jnp.pad(gates, ((0, 0), (0, model_width - 2 * chunk)))
    back_b = jnp.concatenate(
        [back_b.reshape(peer_count, chunk, model_width)[:, :gate_row], gates[:, None, :]], axis=1
    )
    returned_b = lax.all_to_all(back_b, "expert", 0, 0, tiled=True)
    gate_table = returned_b[:, gate_row, : 2 * chunk].reshape(-1)
    returned_b = returned_b.reshape(rows, model_width)

    def weighted(weights, returned):
        return jnp.dot(
            weights,
            returned.astype(jnp.float32),
            precision=lax.Precision.HIGHEST,
            preferred_element_type=jnp.float32,
        )

    combined = grad_tokens.astype(jnp.float32) + weighted(weights_a, returned_a)
    combined = combined + weighted(weights_b, returned_b)
    gate_slot = gate_table[(ids * 2 * chunk + places).reshape(-1)].reshape(token_count, top_count)
    passed = passed_along(combined.astype(jnp.bfloat16), "pipe", -1)
    return (passed[None], gate_slot[None])


def solution(mesh):
    placed = (
        P("pipe", "expert", None),
        P("pipe", "expert", None),
        P("pipe", "expert", None),
        P("pipe", "expert", None),
        P("pipe", "expert", None, None),
        P("pipe", "expert", None, None),
        P("pipe", "expert", None, None),
    )
    return jax.shard_map(
        body,
        mesh=mesh,
        in_specs=placed,
        out_specs=(P("pipe", "expert", None), P("pipe", "expert", None)),
        check_vma=False,
    )
```

```python
import jax
import jax.numpy as jnp
from jax import lax
from jax.sharding import PartitionSpec as P


def passed_along(value, axis, steps):
    count = lax.axis_size(axis)
    first, last = (max(0, -steps), min(count, count - steps))
    return lax.ppermute(value, axis, [(source, source + steps) for source in range(first, last)])


def expert_rows(grad_rows, input_rows, gate_matrix, up_matrix, down_matrix):
    gate_pre = jnp.dot(input_rows, gate_matrix, preferred_element_type=jnp.float32)
    up_pre = jnp.dot(input_rows, up_matrix, preferred_element_type=jnp.float32)
    hidden_grad = lax.dot_general(
        grad_rows, down_matrix, (((1,), (1,)), ((), ())), preferred_element_type=jnp.float32
    )
    sigmoid = jax.nn.sigmoid(gate_pre)
    active = gate_pre * sigmoid
    gate_value = jnp.sum(hidden_grad * active * up_pre, axis=-1).astype(jnp.bfloat16)
    gate_part = (hidden_grad * up_pre * sigmoid * (1.0 + gate_pre * (1.0 - sigmoid))).astype(
        jnp.bfloat16
    )
    up_part = (hidden_grad * active).astype(jnp.bfloat16)
    input_back = lax.dot_general(
        gate_part, gate_matrix, (((1,), (1,)), ((), ())), preferred_element_type=jnp.float32
    ) + lax.dot_general(
        up_part, up_matrix, (((1,), (1,)), ((), ())), preferred_element_type=jnp.float32
    )
    return input_back.astype(jnp.bfloat16), gate_value


def body(out_grad, layer_input, route_ids, route_probs, gate_weight, up_weight, down_weight):
    grad_tokens = out_grad[0]
    input_tokens = layer_input[0]
    chosen = route_ids[0]
    slot_probs = route_probs[0]
    gate_matrix = gate_weight[0, 0]
    up_matrix = up_weight[0, 0]
    down_matrix = down_weight[0, 0]
    peer_count = lax.axis_size("expert")
    token_count, top_count = chosen.shape
    model_width = grad_tokens.shape[1]
    capacity = min(token_count, 7 * token_count * top_count // (6 * peer_count))
    chunk = -(-(capacity + 1) // 16) * 8
    rows = peer_count * chunk

    flat_ids = chosen.reshape(-1)
    one_hot = (flat_ids[:, None] == jnp.arange(peer_count, dtype=jnp.int32)[None, :]).astype(
        jnp.int32
    )
    places = (jnp.sum(one_hot * jnp.cumsum(one_hot, axis=0), axis=1) - 1).reshape(
        token_count, top_count
    )
    ids = chosen
    lanes = jnp.arange(rows, dtype=jnp.int32)[None, None, :]
    both = jnp.concatenate([grad_tokens, input_tokens], axis=1)
    gate_row = chunk - 1

    def dispatch(part):
        local = places - part * chunk
        inside = (local >= 0) & (local < chunk)
        target = jnp.where(inside, ids * chunk + local, -1)
        hits = target[:, :, None] == lanes
        pick = jnp.any(hits, axis=1).astype(jnp.bfloat16)
        send = lax.dot_general(
            pick, both, (((0,), (0,)), ((), ())), preferred_element_type=jnp.float32
        ).astype(jnp.bfloat16)
        weights = jnp.sum(jnp.where(hits, slot_probs[:, :, None], 0.0), axis=1)
        return send.reshape(peer_count, chunk, 2 * model_width), weights

    send_a, weights_a = dispatch(0)
    send_b, weights_b = dispatch(1)
    arrived_a = lax.all_to_all(send_a, "expert", 0, 0, tiled=True).reshape(rows, 2 * model_width)
    arrived_b = lax.all_to_all(send_b, "expert", 0, 0, tiled=True).reshape(rows, 2 * model_width)
    back_a, gate_a = expert_rows(
        arrived_a[:, :model_width], arrived_a[:, model_width:], gate_matrix, up_matrix, down_matrix
    )
    back_a, gate_a, arrived_b = lax.optimization_barrier((back_a, gate_a, arrived_b))
    returned_a = lax.all_to_all(
        back_a.reshape(peer_count, chunk, model_width), "expert", 0, 0, tiled=True
    ).reshape(rows, model_width)
    back_b, gate_b = expert_rows(
        arrived_b[:, :model_width], arrived_b[:, model_width:], gate_matrix, up_matrix, down_matrix
    )
    gates = jnp.concatenate(
        [gate_a.reshape(peer_count, chunk), gate_b.reshape(peer_count, chunk)], axis=1
    )
    gates = jnp.pad(gates, ((0, 0), (0, model_width - 2 * chunk)))
    back_b = jnp.concatenate(
        [back_b.reshape(peer_count, chunk, model_width)[:, :gate_row], gates[:, None, :]], axis=1
    )
    returned_b = lax.all_to_all(back_b, "expert", 0, 0, tiled=True)
    gate_table = returned_b[:, gate_row, : 2 * chunk].reshape(-1)
    returned_b = returned_b.reshape(rows, model_width)

    def weighted(weights, returned):
        return jnp.dot(
            weights,
            returned.astype(jnp.float32),
            precision=lax.Precision.HIGHEST,
            preferred_element_type=jnp.float32,
        )

    combined = grad_tokens.astype(jnp.float32) + weighted(weights_a, returned_a)
    combined = combined + weighted(weights_b, returned_b)
    gate_index = ids * 2 * chunk + places
    gate_hits = gate_index[:, :, None] == jnp.arange(gate_table.shape[0], dtype=jnp.int32)
    gate_slot = jnp.sum(
        jnp.where(gate_hits, gate_table.astype(jnp.float32), 0.0), axis=2
    ).astype(jnp.bfloat16)
    passed = passed_along(combined.astype(jnp.bfloat16), "pipe", -1)
    return (passed[None], gate_slot[None])


def solution(mesh):
    placed = (
        P("pipe", "expert", None),
        P("pipe", "expert", None),
        P("pipe", "expert", None),
        P("pipe", "expert", None),
        P("pipe", "expert", None, None),
        P("pipe", "expert", None, None),
        P("pipe", "expert", None, None),
    )
    return jax.shard_map(
        body,
        mesh=mesh,
        in_specs=placed,
        out_specs=(P("pipe", "expert", None), P("pipe", "expert", None)),
        check_vma=False,
    )
```

```python
import jax
import jax.numpy as jnp
from jax import lax
from jax.experimental import pallas as pl
from jax.sharding import PartitionSpec as P


def passed_along(value, axis, steps):
    count = lax.axis_size(axis)
    first, last = (max(0, -steps), min(count, count - steps))
    return lax.ppermute(value, axis, [(source, source + steps) for source in range(first, last)])


def expert_rows(grad_rows, input_rows, gate_matrix, up_matrix, down_matrix):
    gate_pre = jnp.dot(input_rows, gate_matrix, preferred_element_type=jnp.float32)
    up_pre = jnp.dot(input_rows, up_matrix, preferred_element_type=jnp.float32)
    hidden_grad = lax.dot_general(
        grad_rows, down_matrix, (((1,), (1,)), ((), ())), preferred_element_type=jnp.float32
    )
    sigmoid = jax.nn.sigmoid(gate_pre)
    active = gate_pre * sigmoid
    gate_value = jnp.sum(hidden_grad * active * up_pre, axis=-1).astype(jnp.bfloat16)
    gate_part = (hidden_grad * up_pre * sigmoid * (1.0 + gate_pre * (1.0 - sigmoid))).astype(
        jnp.bfloat16
    )
    up_part = (hidden_grad * active).astype(jnp.bfloat16)
    input_back = lax.dot_general(
        gate_part, gate_matrix, (((1,), (1,)), ((), ())), preferred_element_type=jnp.float32
    ) + lax.dot_general(
        up_part, up_matrix, (((1,), (1,)), ((), ())), preferred_element_type=jnp.float32
    )
    return input_back.astype(jnp.bfloat16), gate_value


def expert_kernel(grad_ref, input_ref, gate_ref, up_ref, down_ref, back_ref, value_ref):
    grad_rows = grad_ref[...]
    input_rows = input_ref[...]
    gate_matrix = gate_ref[...]
    up_matrix = up_ref[...]
    gate_pre = jnp.dot(input_rows, gate_matrix, preferred_element_type=jnp.float32)
    up_pre = jnp.dot(input_rows, up_matrix, preferred_element_type=jnp.float32)
    hidden_grad = lax.dot_general(
        grad_rows, down_ref[...], (((1,), (1,)), ((), ())), preferred_element_type=jnp.float32
    )
    sigmoid = jax.nn.sigmoid(gate_pre)
    active = gate_pre * sigmoid
    value = jnp.sum(hidden_grad * active * up_pre, axis=-1, keepdims=True)
    value_ref[...] = jnp.broadcast_to(value, value_ref.shape)
    gate_part = (hidden_grad * up_pre * sigmoid * (1.0 + gate_pre * (1.0 - sigmoid))).astype(jnp.bfloat16)
    up_part = (hidden_grad * active).astype(jnp.bfloat16)
    back = lax.dot_general(
        gate_part, gate_matrix, (((1,), (1,)), ((), ())), preferred_element_type=jnp.float32
    ) + lax.dot_general(up_part, up_matrix, (((1,), (1,)), ((), ())), preferred_element_type=jnp.float32)
    back_ref[...] = back.astype(back_ref.dtype)

def expert_call(arrived, gate_matrix, up_matrix, down_matrix, tile=256):
    rows, both = arrived.shape
    width = both // 2
    hidden = gate_matrix.shape[1]
    steps = rows // tile
    flops = 2 * rows * width * hidden * 5
    cost = pl.CostEstimate(flops=flops, transcendentals=rows * hidden,
                           bytes_accessed=rows * both * 2 + 3 * width * hidden * 2 + rows * width * 2)
    back, value = pl.pallas_call(
        expert_kernel,
        grid=(steps,),
        in_specs=[
            pl.BlockSpec((tile, width), lambda i: (i, 0)),
            pl.BlockSpec((tile, width), lambda i: (i, 1)),
            pl.BlockSpec((width, hidden), lambda i: (0, 0)),
            pl.BlockSpec((width, hidden), lambda i: (0, 0)),
            pl.BlockSpec((hidden, width), lambda i: (0, 0)),
        ],
        out_specs=[
            pl.BlockSpec((tile, width), lambda i: (i, 0)),
            pl.BlockSpec((tile, 128), lambda i: (i, 0)),
        ],
        out_shape=[
            jax.ShapeDtypeStruct((rows, width), jnp.bfloat16),
            jax.ShapeDtypeStruct((rows, 128), jnp.float32),
        ],
        cost_estimate=cost,
    )(arrived, arrived, gate_matrix, up_matrix, down_matrix)
    return back, value[:, 0].astype(jnp.bfloat16)


def body(out_grad, layer_input, route_ids, route_probs, gate_weight, up_weight, down_weight):
    grad_tokens = out_grad[0]
    input_tokens = layer_input[0]
    chosen = route_ids[0]
    slot_probs = route_probs[0]
    gate_matrix = gate_weight[0, 0]
    up_matrix = up_weight[0, 0]
    down_matrix = down_weight[0, 0]
    peer_count = lax.axis_size("expert")
    token_count, top_count = chosen.shape
    model_width = grad_tokens.shape[1]
    capacity = min(token_count, 7 * token_count * top_count // (6 * peer_count))
    chunk = -(-(capacity + 1) // 16) * 8
    rows = peer_count * chunk

    flat_ids = chosen.reshape(-1)
    one_hot = (flat_ids[:, None] == jnp.arange(peer_count, dtype=jnp.int32)[None, :]).astype(
        jnp.int32
    )
    places = (jnp.sum(one_hot * jnp.cumsum(one_hot, axis=0), axis=1) - 1).reshape(
        token_count, top_count
    )
    ids = chosen
    lanes = jnp.arange(rows, dtype=jnp.int32)[None, None, :]
    both = jnp.concatenate([grad_tokens, input_tokens], axis=1)
    gate_row = chunk - 1

    def dispatch(part):
        local = places - part * chunk
        inside = (local >= 0) & (local < chunk)
        target = jnp.where(inside, ids * chunk + local, -1)
        hits = target[:, :, None] == lanes
        pick = jnp.any(hits, axis=1).astype(jnp.bfloat16)
        send = lax.dot_general(
            pick, both, (((0,), (0,)), ((), ())), preferred_element_type=jnp.float32
        ).astype(jnp.bfloat16)
        weights = jnp.sum(jnp.where(hits, slot_probs[:, :, None], 0.0), axis=1)
        return send.reshape(peer_count, chunk, 2 * model_width), weights

    send_a, weights_a = dispatch(0)
    send_b, weights_b = dispatch(1)
    arrived_a = lax.all_to_all(send_a, "expert", 0, 0, tiled=True).reshape(rows, 2 * model_width)
    arrived_b = lax.all_to_all(send_b, "expert", 0, 0, tiled=True).reshape(rows, 2 * model_width)
    back_a, gate_a = expert_call(arrived_a, gate_matrix, up_matrix, down_matrix)
    back_a, gate_a, arrived_b = lax.optimization_barrier((back_a, gate_a, arrived_b))
    returned_a = lax.all_to_all(
        back_a.reshape(peer_count, chunk, model_width), "expert", 0, 0, tiled=True
    ).reshape(rows, model_width)
    back_b, gate_b = expert_call(arrived_b, gate_matrix, up_matrix, down_matrix)
    gates = jnp.concatenate(
        [gate_a.reshape(peer_count, chunk), gate_b.reshape(peer_count, chunk)], axis=1
    )
    gates = jnp.pad(gates, ((0, 0), (0, model_width - 2 * chunk)))
    back_b = jnp.concatenate(
        [back_b.reshape(peer_count, chunk, model_width)[:, :gate_row], gates[:, None, :]], axis=1
    )
    returned_b = lax.all_to_all(back_b, "expert", 0, 0, tiled=True)
    gate_table = returned_b[:, gate_row, : 2 * chunk].reshape(-1)
    returned_b = returned_b.reshape(rows, model_width)

    def weighted(weights, returned):
        return jnp.dot(
            weights,
            returned.astype(jnp.float32),
            precision=lax.Precision.HIGHEST,
            preferred_element_type=jnp.float32,
        )

    combined = grad_tokens.astype(jnp.float32) + weighted(weights_a, returned_a)
    combined = combined + weighted(weights_b, returned_b)
    gate_index = ids * 2 * chunk + places
    gate_hits = gate_index[:, :, None] == jnp.arange(gate_table.shape[0], dtype=jnp.int32)
    gate_slot = jnp.sum(
        jnp.where(gate_hits, gate_table.astype(jnp.float32), 0.0), axis=2
    ).astype(jnp.bfloat16)
    passed = passed_along(combined.astype(jnp.bfloat16)[None], "pipe", -1)
    return (passed, gate_slot[None])


def solution(mesh):
    placed = (
        P("pipe", "expert", None),
        P("pipe", "expert", None),
        P("pipe", "expert", None),
        P("pipe", "expert", None),
        P("pipe", "expert", None, None),
        P("pipe", "expert", None, None),
        P("pipe", "expert", None, None),
    )
    return jax.shard_map(
        body,
        mesh=mesh,
        in_specs=placed,
        out_specs=(P("pipe", "expert", None), P("pipe", "expert", None)),
        check_vma=False,
    )
```

```python
import jax
import jax.numpy as jnp
from jax import lax
from jax.experimental import pallas as pl
from jax.sharding import PartitionSpec as P


def passed_along(value, axis, steps):
    count = lax.axis_size(axis)
    first, last = (max(0, -steps), min(count, count - steps))
    return lax.ppermute(value, axis, [(source, source + steps) for source in range(first, last)])


def expert_rows(grad_rows, input_rows, gate_matrix, up_matrix, down_matrix):
    gate_pre = jnp.dot(input_rows, gate_matrix, preferred_element_type=jnp.float32)
    up_pre = jnp.dot(input_rows, up_matrix, preferred_element_type=jnp.float32)
    hidden_grad = lax.dot_general(
        grad_rows, down_matrix, (((1,), (1,)), ((), ())), preferred_element_type=jnp.float32
    )
    sigmoid = jax.nn.sigmoid(gate_pre)
    active = gate_pre * sigmoid
    gate_value = jnp.sum(hidden_grad * active * up_pre, axis=-1).astype(jnp.bfloat16)
    gate_part = (hidden_grad * up_pre * sigmoid * (1.0 + gate_pre * (1.0 - sigmoid))).astype(
        jnp.bfloat16
    )
    up_part = (hidden_grad * active).astype(jnp.bfloat16)
    input_back = lax.dot_general(
        gate_part, gate_matrix, (((1,), (1,)), ((), ())), preferred_element_type=jnp.float32
    ) + lax.dot_general(
        up_part, up_matrix, (((1,), (1,)), ((), ())), preferred_element_type=jnp.float32
    )
    return input_back.astype(jnp.bfloat16), gate_value


def expert_kernel(grad_ref, input_ref, gate_ref, up_ref, down_ref, back_ref, value_ref):
    grad_rows = grad_ref[...]
    input_rows = input_ref[...]
    gate_matrix = gate_ref[...]
    up_matrix = up_ref[...]
    gate_pre = jnp.dot(input_rows, gate_matrix, preferred_element_type=jnp.float32)
    up_pre = jnp.dot(input_rows, up_matrix, preferred_element_type=jnp.float32)
    hidden_grad = lax.dot_general(
        grad_rows, down_ref[...], (((1,), (1,)), ((), ())), preferred_element_type=jnp.float32
    )
    sigmoid = jax.nn.sigmoid(gate_pre)
    active = gate_pre * sigmoid
    value = jnp.sum(hidden_grad * active * up_pre, axis=-1, keepdims=True)
    value_ref[...] = jnp.broadcast_to(value, value_ref.shape)
    gate_part = (hidden_grad * up_pre * sigmoid * (1.0 + gate_pre * (1.0 - sigmoid))).astype(jnp.bfloat16)
    up_part = (hidden_grad * active).astype(jnp.bfloat16)
    back = lax.dot_general(
        gate_part, gate_matrix, (((1,), (1,)), ((), ())), preferred_element_type=jnp.float32
    ) + lax.dot_general(up_part, up_matrix, (((1,), (1,)), ((), ())), preferred_element_type=jnp.float32)
    back_ref[...] = back.astype(back_ref.dtype)

def expert_call(arrived, gate_matrix, up_matrix, down_matrix, tile=256):
    rows, both = arrived.shape
    width = both // 2
    hidden = gate_matrix.shape[1]
    steps = rows // tile
    flops = 2 * rows * width * hidden * 5
    cost = pl.CostEstimate(flops=flops, transcendentals=rows * hidden,
                           bytes_accessed=rows * both * 2 + 3 * width * hidden * 2 + rows * width * 2)
    back, value = pl.pallas_call(
        expert_kernel,
        grid=(steps,),
        in_specs=[
            pl.BlockSpec((tile, width), lambda i: (i, 0)),
            pl.BlockSpec((tile, width), lambda i: (i, 1)),
            pl.BlockSpec((width, hidden), lambda i: (0, 0)),
            pl.BlockSpec((width, hidden), lambda i: (0, 0)),
            pl.BlockSpec((hidden, width), lambda i: (0, 0)),
        ],
        out_specs=[
            pl.BlockSpec((tile, width), lambda i: (i, 0)),
            pl.BlockSpec((tile, 128), lambda i: (i, 0)),
        ],
        out_shape=[
            jax.ShapeDtypeStruct((rows, width), jnp.bfloat16),
            jax.ShapeDtypeStruct((rows, 128), jnp.float32),
        ],
        cost_estimate=cost,
    )(arrived, arrived, gate_matrix, up_matrix, down_matrix)
    return back, value[:, 0].astype(jnp.bfloat16)


def body(out_grad, layer_input, route_ids, route_probs, gate_weight, up_weight, down_weight):
    grad_tokens = out_grad[0]
    input_tokens = layer_input[0]
    chosen = route_ids[0]
    slot_probs = route_probs[0]
    gate_matrix = gate_weight[0, 0]
    up_matrix = up_weight[0, 0]
    down_matrix = down_weight[0, 0]
    peer_count = lax.axis_size("expert")
    token_count, top_count = chosen.shape
    model_width = grad_tokens.shape[1]
    capacity = min(token_count, 7 * token_count * top_count // (6 * peer_count))
    chunk = -(-(capacity + 1) // 16) * 8
    rows = peer_count * chunk

    flat_ids = chosen.reshape(-1)
    one_hot = (flat_ids[:, None] == jnp.arange(peer_count, dtype=jnp.int32)[None, :]).astype(
        jnp.int32
    )
    places = (jnp.sum(one_hot * jnp.cumsum(one_hot, axis=0), axis=1) - 1).reshape(
        token_count, top_count
    )
    ids = chosen
    lanes = jnp.arange(rows, dtype=jnp.int32)[None, None, :]
    both = jnp.concatenate([grad_tokens, input_tokens], axis=1)
    gate_row = chunk - 1

    def dispatch(part):
        local = places - part * chunk
        inside = (local >= 0) & (local < chunk)
        target = jnp.where(inside, ids * chunk + local, -1)
        hits = target[:, :, None] == lanes
        pick = jnp.any(target[None, :, :] == lanes.reshape(rows, 1, 1), axis=2)
        send = jnp.dot(
            pick.astype(jnp.bfloat16), both, preferred_element_type=jnp.float32
        ).astype(jnp.bfloat16)
        weights = jnp.sum(jnp.where(hits, slot_probs[:, :, None], 0.0), axis=1)
        return send.reshape(peer_count, chunk, 2 * model_width), weights

    send_a, weights_a = dispatch(0)
    send_b, weights_b = dispatch(1)
    arrived_a = lax.all_to_all(send_a, "expert", 0, 0, tiled=True).reshape(rows, 2 * model_width)
    arrived_b = lax.all_to_all(send_b, "expert", 0, 0, tiled=True).reshape(rows, 2 * model_width)
    back_a, gate_a = expert_call(arrived_a, gate_matrix, up_matrix, down_matrix)
    back_a, gate_a, arrived_b = lax.optimization_barrier((back_a, gate_a, arrived_b))
    returned_a = lax.all_to_all(
        back_a.reshape(peer_count, chunk, model_width), "expert", 0, 0, tiled=True
    ).reshape(rows, model_width)
    back_b, gate_b = expert_call(arrived_b, gate_matrix, up_matrix, down_matrix)
    gates = jnp.concatenate(
        [gate_a.reshape(peer_count, chunk), gate_b.reshape(peer_count, chunk)], axis=1
    )
    gates = jnp.pad(gates, ((0, 0), (0, model_width - 2 * chunk)))
    back_b = jnp.concatenate(
        [back_b.reshape(peer_count, chunk, model_width)[:, :gate_row], gates[:, None, :]], axis=1
    )
    returned_b = lax.all_to_all(back_b, "expert", 0, 0, tiled=True)
    gate_table = returned_b[:, gate_row, : 2 * chunk].reshape(-1)
    returned_b = returned_b.reshape(rows, model_width)

    def weighted(weights, returned):
        return jnp.dot(
            weights,
            returned.astype(jnp.float32),
            precision=lax.Precision.HIGHEST,
            preferred_element_type=jnp.float32,
        )

    combined = grad_tokens.astype(jnp.float32) + weighted(weights_a, returned_a)
    combined = combined + weighted(weights_b, returned_b)
    gate_index = ids * 2 * chunk + places
    gate_hits = gate_index[:, :, None] == jnp.arange(gate_table.shape[0], dtype=jnp.int32)
    gate_slot = jnp.sum(
        jnp.where(gate_hits, gate_table.astype(jnp.float32), 0.0), axis=2
    ).astype(jnp.bfloat16)
    passed = passed_along(combined.astype(jnp.bfloat16)[None], "pipe", -1)
    return (passed, gate_slot[None])


def solution(mesh):
    placed = (
        P("pipe", "expert", None),
        P("pipe", "expert", None),
        P("pipe", "expert", None),
        P("pipe", "expert", None),
        P("pipe", "expert", None, None),
        P("pipe", "expert", None, None),
        P("pipe", "expert", None, None),
    )
    return jax.shard_map(
        body,
        mesh=mesh,
        in_specs=placed,
        out_specs=(P("pipe", "expert", None), P("pipe", "expert", None)),
        check_vma=False,
    )
```

```python
import jax
import jax.numpy as jnp
from jax import lax
from jax.experimental import pallas as pl
from jax.sharding import PartitionSpec as P


def passed_along(value, axis, steps):
    count = lax.axis_size(axis)
    first, last = (max(0, -steps), min(count, count - steps))
    return lax.ppermute(value, axis, [(source, source + steps) for source in range(first, last)])


def expert_rows(grad_rows, input_rows, gate_matrix, up_matrix, down_matrix):
    gate_pre = jnp.dot(input_rows, gate_matrix, preferred_element_type=jnp.float32)
    up_pre = jnp.dot(input_rows, up_matrix, preferred_element_type=jnp.float32)
    hidden_grad = lax.dot_general(
        grad_rows, down_matrix, (((1,), (1,)), ((), ())), preferred_element_type=jnp.float32
    )
    sigmoid = jax.nn.sigmoid(gate_pre)
    active = gate_pre * sigmoid
    gate_value = jnp.sum(hidden_grad * active * up_pre, axis=-1).astype(jnp.bfloat16)
    gate_part = (hidden_grad * up_pre * sigmoid * (1.0 + gate_pre * (1.0 - sigmoid))).astype(
        jnp.bfloat16
    )
    up_part = (hidden_grad * active).astype(jnp.bfloat16)
    input_back = lax.dot_general(
        gate_part, gate_matrix, (((1,), (1,)), ((), ())), preferred_element_type=jnp.float32
    ) + lax.dot_general(
        up_part, up_matrix, (((1,), (1,)), ((), ())), preferred_element_type=jnp.float32
    )
    return input_back.astype(jnp.bfloat16), gate_value


def expert_kernel(grad_ref, input_ref, gate_ref, up_ref, down_ref, back_ref, value_ref):
    grad_rows = grad_ref[...]
    input_rows = input_ref[...]
    gate_matrix = gate_ref[...]
    up_matrix = up_ref[...]
    gate_pre = jnp.dot(input_rows, gate_matrix, preferred_element_type=jnp.float32)
    up_pre = jnp.dot(input_rows, up_matrix, preferred_element_type=jnp.float32)
    hidden_grad = lax.dot_general(
        grad_rows, down_ref[...], (((1,), (1,)), ((), ())), preferred_element_type=jnp.float32
    )
    sigmoid = jax.nn.sigmoid(gate_pre)
    active = gate_pre * sigmoid
    value = jnp.sum(hidden_grad * active * up_pre, axis=-1, keepdims=True)
    value_ref[...] = jnp.broadcast_to(value, value_ref.shape)
    gate_part = (hidden_grad * up_pre * sigmoid * (1.0 + gate_pre * (1.0 - sigmoid))).astype(jnp.bfloat16)
    up_part = (hidden_grad * active).astype(jnp.bfloat16)
    back = lax.dot_general(
        gate_part, gate_matrix, (((1,), (1,)), ((), ())), preferred_element_type=jnp.float32
    ) + lax.dot_general(up_part, up_matrix, (((1,), (1,)), ((), ())), preferred_element_type=jnp.float32)
    back_ref[...] = back.astype(back_ref.dtype)

def expert_call(arrived, gate_matrix, up_matrix, down_matrix, tile=256):
    rows, both = arrived.shape
    width = both // 2
    hidden = gate_matrix.shape[1]
    steps = rows // tile
    flops = 2 * rows * width * hidden * 5
    cost = pl.CostEstimate(flops=flops, transcendentals=rows * hidden,
                           bytes_accessed=rows * both * 2 + 3 * width * hidden * 2 + rows * width * 2)
    back, value = pl.pallas_call(
        expert_kernel,
        grid=(steps,),
        in_specs=[
            pl.BlockSpec((tile, width), lambda i: (i, 0)),
            pl.BlockSpec((tile, width), lambda i: (i, 1)),
            pl.BlockSpec((width, hidden), lambda i: (0, 0)),
            pl.BlockSpec((width, hidden), lambda i: (0, 0)),
            pl.BlockSpec((hidden, width), lambda i: (0, 0)),
        ],
        out_specs=[
            pl.BlockSpec((tile, width), lambda i: (i, 0)),
            pl.BlockSpec((tile, 128), lambda i: (i, 0)),
        ],
        out_shape=[
            jax.ShapeDtypeStruct((rows, width), jnp.bfloat16),
            jax.ShapeDtypeStruct((rows, 128), jnp.float32),
        ],
        cost_estimate=cost,
    )(arrived, arrived, gate_matrix, up_matrix, down_matrix)
    return back, value[:, 0].astype(jnp.bfloat16)


def body(out_grad, layer_input, route_ids, route_probs, gate_weight, up_weight, down_weight):
    grad_tokens = out_grad[0]
    input_tokens = layer_input[0]
    chosen = route_ids[0]
    slot_probs = route_probs[0]
    gate_matrix = gate_weight[0, 0]
    up_matrix = up_weight[0, 0]
    down_matrix = down_weight[0, 0]
    peer_count = lax.axis_size("expert")
    token_count, top_count = chosen.shape
    model_width = grad_tokens.shape[1]
    capacity = min(token_count, 7 * token_count * top_count // (6 * peer_count))
    chunk = -(-(capacity + 1) // 16) * 8
    rows = peer_count * chunk

    flat_ids = chosen.reshape(-1)
    one_hot = (flat_ids[:, None] == jnp.arange(peer_count, dtype=jnp.int32)[None, :]).astype(
        jnp.int32
    )
    places = (jnp.sum(one_hot * jnp.cumsum(one_hot, axis=0), axis=1) - 1).reshape(
        token_count, top_count
    )
    ids = chosen
    lanes = jnp.arange(rows, dtype=jnp.int32)[None, None, :]
    both = jnp.concatenate([grad_tokens, input_tokens], axis=1)

    def dispatch(part):
        local = places - part * chunk
        inside = (local >= 0) & (local < chunk)
        target = jnp.where(inside, ids * chunk + local, -1)
        hits = target[:, :, None] == lanes
        pick = jnp.any(target[None, :, :] == lanes.reshape(rows, 1, 1), axis=2)
        weights = jnp.sum(jnp.where(hits, slot_probs[:, :, None], 0.0), axis=1)
        return pick, weights

    pick_a, weights_a = dispatch(0)
    send_a = jnp.dot(pick_a.astype(jnp.bfloat16), both, preferred_element_type=jnp.float32)
    send_a = send_a.astype(jnp.bfloat16).reshape(peer_count, chunk, 2 * model_width)
    unused, weights_b = dispatch(1)
    rest = capacity - chunk
    local = places - chunk
    grad_row = jnp.where(local >= 0, ids * 2 * rest + local, -1)
    input_row = jnp.where(local >= 0, grad_row + rest, -1)
    send_lanes = jnp.arange(peer_count * 2 * rest, dtype=jnp.int32).reshape(-1, 1, 1)
    pick_grad = jnp.any(grad_row[None, :, :] == send_lanes, axis=2).astype(jnp.bfloat16)
    pick_input = jnp.any(input_row[None, :, :] == send_lanes, axis=2).astype(jnp.bfloat16)
    send_b = jnp.dot(pick_grad, grad_tokens, preferred_element_type=jnp.float32) + jnp.dot(
        pick_input, input_tokens, preferred_element_type=jnp.float32
    )
    send_b = send_b.astype(jnp.bfloat16).reshape(peer_count, 2 * rest, model_width)

    arrived_a = lax.all_to_all(send_a, "expert", 0, 0, tiled=True).reshape(rows, 2 * model_width)
    arrived_b = lax.all_to_all(send_b, "expert", 0, 0, tiled=True)
    back_a, gate_a = expert_call(arrived_a, gate_matrix, up_matrix, down_matrix)
    back_a, gate_a, arrived_b = lax.optimization_barrier((back_a, gate_a, arrived_b))
    returned_a = lax.all_to_all(
        back_a.reshape(peer_count, chunk, model_width), "expert", 0, 0, tiled=True
    ).reshape(rows, model_width)
    arrived_b = jnp.concatenate(
        [
            arrived_b[:, :rest].reshape(peer_count * rest, model_width),
            arrived_b[:, rest:].reshape(peer_count * rest, model_width),
        ],
        axis=1,
    )
    back_b, gate_b = expert_call(arrived_b, gate_matrix, up_matrix, down_matrix, tile=128)
    gates = jnp.concatenate(
        [gate_a.reshape(peer_count, chunk), gate_b.reshape(peer_count, rest)], axis=1
    )
    gates = jnp.pad(gates, ((0, 0), (0, model_width - capacity)))
    back_b = jnp.concatenate(
        [
            back_b.reshape(peer_count, rest, model_width),
            gates[:, None, :],
            jnp.zeros((peer_count, chunk - rest - 1, model_width), back_b.dtype),
        ],
        axis=1,
    )
    returned_b = lax.all_to_all(back_b, "expert", 0, 0, tiled=True)
    gate_table = returned_b[:, rest, :capacity].reshape(-1)
    returned_b = returned_b.reshape(rows, model_width)

    def weighted(weights, returned):
        return jnp.dot(
            weights,
            returned.astype(jnp.float32),
            precision=lax.Precision.HIGHEST,
            preferred_element_type=jnp.float32,
        )

    combined = grad_tokens.astype(jnp.float32) + weighted(weights_a, returned_a)
    combined = combined + weighted(weights_b, returned_b)
    gate_index = ids * capacity + places
    gate_hits = gate_index[:, :, None] == jnp.arange(gate_table.shape[0], dtype=jnp.int32)
    gate_slot = jnp.sum(
        jnp.where(gate_hits, gate_table.astype(jnp.float32), 0.0), axis=2
    ).astype(jnp.bfloat16)
    passed = passed_along(combined.astype(jnp.bfloat16)[None], "pipe", -1)
    return (passed, gate_slot[None])


def solution(mesh):
    placed = (
        P("pipe", "expert", None),
        P("pipe", "expert", None),
        P("pipe", "expert", None),
        P("pipe", "expert", None),
        P("pipe", "expert", None, None),
        P("pipe", "expert", None, None),
        P("pipe", "expert", None, None),
    )
    return jax.shard_map(
        body,
        mesh=mesh,
        in_specs=placed,
        out_specs=(P("pipe", "expert", None), P("pipe", "expert", None)),
        check_vma=False,
    )
```

```python
import jax
import jax.numpy as jnp
from jax import lax
from jax.experimental import pallas as pl
from jax.sharding import PartitionSpec as P


def passed_along(value, axis, steps):
    count = lax.axis_size(axis)
    first, last = (max(0, -steps), min(count, count - steps))
    return lax.ppermute(value, axis, [(source, source + steps) for source in range(first, last)])


def expert_rows(grad_rows, input_rows, gate_matrix, up_matrix, down_matrix):
    gate_pre = jnp.dot(input_rows, gate_matrix, preferred_element_type=jnp.float32)
    up_pre = jnp.dot(input_rows, up_matrix, preferred_element_type=jnp.float32)
    hidden_grad = lax.dot_general(
        grad_rows, down_matrix, (((1,), (1,)), ((), ())), preferred_element_type=jnp.float32
    )
    sigmoid = jax.nn.sigmoid(gate_pre)
    active = gate_pre * sigmoid
    gate_value = jnp.sum(hidden_grad * active * up_pre, axis=-1).astype(jnp.bfloat16)
    gate_part = (hidden_grad * up_pre * sigmoid * (1.0 + gate_pre * (1.0 - sigmoid))).astype(
        jnp.bfloat16
    )
    up_part = (hidden_grad * active).astype(jnp.bfloat16)
    input_back = lax.dot_general(
        gate_part, gate_matrix, (((1,), (1,)), ((), ())), preferred_element_type=jnp.float32
    ) + lax.dot_general(
        up_part, up_matrix, (((1,), (1,)), ((), ())), preferred_element_type=jnp.float32
    )
    return input_back.astype(jnp.bfloat16), gate_value


def expert_kernel(grad_ref, input_ref, gate_ref, up_ref, down_ref, back_ref, value_ref):
    grad_rows = grad_ref[...]
    input_rows = input_ref[...]
    gate_matrix = gate_ref[...]
    up_matrix = up_ref[...]
    gate_pre = jnp.dot(input_rows, gate_matrix, preferred_element_type=jnp.float32)
    up_pre = jnp.dot(input_rows, up_matrix, preferred_element_type=jnp.float32)
    hidden_grad = lax.dot_general(
        grad_rows, down_ref[...], (((1,), (1,)), ((), ())), preferred_element_type=jnp.float32
    )
    sigmoid = jax.nn.sigmoid(gate_pre)
    active = gate_pre * sigmoid
    value = jnp.sum(hidden_grad * active * up_pre, axis=-1, keepdims=True)
    value_ref[...] = jnp.broadcast_to(value, value_ref.shape)
    gate_part = (hidden_grad * up_pre * sigmoid * (1.0 + gate_pre * (1.0 - sigmoid))).astype(jnp.bfloat16)
    up_part = (hidden_grad * active).astype(jnp.bfloat16)
    back = lax.dot_general(
        gate_part, gate_matrix, (((1,), (1,)), ((), ())), preferred_element_type=jnp.float32
    ) + lax.dot_general(up_part, up_matrix, (((1,), (1,)), ((), ())), preferred_element_type=jnp.float32)
    back_ref[...] = back.astype(back_ref.dtype)

def expert_call(arrived, gate_matrix, up_matrix, down_matrix, tile=256):
    rows, both = arrived.shape
    width = both // 2
    hidden = gate_matrix.shape[1]
    steps = rows // tile
    flops = 2 * rows * width * hidden * 5
    cost = pl.CostEstimate(flops=flops, transcendentals=rows * hidden,
                           bytes_accessed=rows * both * 2 + 3 * width * hidden * 2 + rows * width * 2)
    back, value = pl.pallas_call(
        expert_kernel,
        grid=(steps,),
        in_specs=[
            pl.BlockSpec((tile, width), lambda i: (i, 0)),
            pl.BlockSpec((tile, width), lambda i: (i, 1)),
            pl.BlockSpec((width, hidden), lambda i: (0, 0)),
            pl.BlockSpec((width, hidden), lambda i: (0, 0)),
            pl.BlockSpec((hidden, width), lambda i: (0, 0)),
        ],
        out_specs=[
            pl.BlockSpec((tile, width), lambda i: (i, 0)),
            pl.BlockSpec((tile, 128), lambda i: (i, 0)),
        ],
        out_shape=[
            jax.ShapeDtypeStruct((rows, width), jnp.bfloat16),
            jax.ShapeDtypeStruct((rows, 128), jnp.float32),
        ],
        cost_estimate=cost,
    )(arrived, arrived, gate_matrix, up_matrix, down_matrix)
    return back, value[:, 0].astype(jnp.bfloat16)


def body(out_grad, layer_input, route_ids, route_probs, gate_weight, up_weight, down_weight):
    grad_tokens = out_grad[0]
    input_tokens = layer_input[0]
    chosen = route_ids[0]
    slot_probs = route_probs[0]
    gate_matrix = gate_weight[0, 0]
    up_matrix = up_weight[0, 0]
    down_matrix = down_weight[0, 0]
    peer_count = lax.axis_size("expert")
    token_count, top_count = chosen.shape
    model_width = grad_tokens.shape[1]
    capacity = min(token_count, 7 * token_count * top_count // (6 * peer_count))
    chunk = -(-(capacity + 1) // 16) * 8
    rows = peer_count * chunk

    flat_ids = chosen.reshape(-1)
    one_hot = (flat_ids[:, None] == jnp.arange(peer_count, dtype=jnp.int32)[None, :]).astype(
        jnp.int32
    )
    places = (jnp.sum(one_hot * jnp.cumsum(one_hot, axis=0), axis=1) - 1).reshape(
        token_count, top_count
    )
    ids = chosen
    lanes = jnp.arange(rows, dtype=jnp.int32)[None, None, :]
    both = jnp.concatenate([grad_tokens, input_tokens], axis=1)

    def dispatch(part):
        local = places - part * chunk
        inside = (local >= 0) & (local < chunk)
        target = jnp.where(inside, ids * chunk + local, -1)
        hits = target[:, :, None] == lanes
        pick = jnp.any(target[None, :, :] == lanes.reshape(rows, 1, 1), axis=2)
        weights = jnp.sum(jnp.where(hits, slot_probs[:, :, None], 0.0), axis=1)
        return pick, weights

    pick_a, weights_a = dispatch(0)
    send_a = jnp.dot(pick_a.astype(jnp.bfloat16), both, preferred_element_type=jnp.float32)
    send_a = send_a.astype(jnp.bfloat16).reshape(peer_count, chunk, 2 * model_width)
    unused, weights_b = dispatch(1)
    rest = capacity - chunk
    local = places - chunk
    grad_row = jnp.where(local >= 0, ids * 2 * rest + local, -1)
    input_row = jnp.where(local >= 0, grad_row + rest, -1)
    send_lanes = jnp.arange(peer_count * 2 * rest, dtype=jnp.int32).reshape(-1, 1, 1)
    pick_grad = jnp.any(grad_row[None, :, :] == send_lanes, axis=2).astype(jnp.bfloat16)
    pick_input = jnp.any(input_row[None, :, :] == send_lanes, axis=2).astype(jnp.bfloat16)
    send_b = jnp.dot(pick_grad, grad_tokens, preferred_element_type=jnp.float32) + jnp.dot(
        pick_input, input_tokens, preferred_element_type=jnp.float32
    )
    send_b = send_b.astype(jnp.bfloat16).reshape(peer_count, 2 * rest, model_width)

    arrived_a = lax.all_to_all(send_a, "expert", 0, 0, tiled=True).reshape(rows, 2 * model_width)
    arrived_b = lax.all_to_all(send_b, "expert", 0, 0, tiled=True)
    back_a, gate_a = expert_call(arrived_a, gate_matrix, up_matrix, down_matrix)
    back_a, gate_a, arrived_b = lax.optimization_barrier((back_a, gate_a, arrived_b))
    returned_a = lax.all_to_all(
        back_a.reshape(peer_count, chunk, model_width), "expert", 0, 0, tiled=True
    ).reshape(rows, model_width)
    arrived_b = (
        arrived_b.reshape(peer_count, 2, rest, model_width)
        .transpose(0, 2, 1, 3)
        .reshape(peer_count * rest, 2 * model_width)
    )
    back_b, gate_b = expert_call(arrived_b, gate_matrix, up_matrix, down_matrix, tile=128)
    gates = jnp.concatenate(
        [gate_a.reshape(peer_count, chunk), gate_b.reshape(peer_count, rest)], axis=1
    )
    gates = jnp.pad(gates, ((0, 0), (0, model_width - capacity)))
    back_b = jnp.concatenate(
        [
            back_b.reshape(peer_count, rest, model_width),
            gates[:, None, :],
            jnp.zeros((peer_count, chunk - rest - 1, model_width), back_b.dtype),
        ],
        axis=1,
    )
    returned_b = lax.all_to_all(back_b, "expert", 0, 0, tiled=True)
    gate_table = returned_b[:, rest, :capacity].reshape(-1)
    returned_b = returned_b.reshape(rows, model_width)

    def weighted(weights, returned):
        return jnp.dot(
            weights,
            returned.astype(jnp.float32),
            precision=lax.Precision.HIGHEST,
            preferred_element_type=jnp.float32,
        )

    combined = grad_tokens.astype(jnp.float32) + weighted(weights_a, returned_a)
    combined = combined + weighted(weights_b, returned_b)
    gate_index = ids * capacity + places
    gate_hits = gate_index[:, :, None] == jnp.arange(gate_table.shape[0], dtype=jnp.int32)
    gate_slot = jnp.sum(
        jnp.where(gate_hits, gate_table.astype(jnp.float32), 0.0), axis=2
    ).astype(jnp.bfloat16)
    passed = passed_along(combined.astype(jnp.bfloat16)[None], "pipe", -1)
    return (passed, gate_slot[None])


def solution(mesh):
    placed = (
        P("pipe", "expert", None),
        P("pipe", "expert", None),
        P("pipe", "expert", None),
        P("pipe", "expert", None),
        P("pipe", "expert", None, None),
        P("pipe", "expert", None, None),
        P("pipe", "expert", None, None),
    )
    return jax.shard_map(
        body,
        mesh=mesh,
        in_specs=placed,
        out_specs=(P("pipe", "expert", None), P("pipe", "expert", None)),
        check_vma=False,
    )
```

```python
import jax
import jax.numpy as jnp
from jax import lax
from jax.experimental import pallas as pl
from jax.sharding import PartitionSpec as P


def passed_along(value, axis, steps):
    count = lax.axis_size(axis)
    first, last = (max(0, -steps), min(count, count - steps))
    return lax.ppermute(value, axis, [(source, source + steps) for source in range(first, last)])


def expert_rows(grad_rows, input_rows, gate_matrix, up_matrix, down_matrix):
    gate_pre = jnp.dot(input_rows, gate_matrix, preferred_element_type=jnp.float32)
    up_pre = jnp.dot(input_rows, up_matrix, preferred_element_type=jnp.float32)
    hidden_grad = lax.dot_general(
        grad_rows, down_matrix, (((1,), (1,)), ((), ())), preferred_element_type=jnp.float32
    )
    sigmoid = jax.nn.sigmoid(gate_pre)
    active = gate_pre * sigmoid
    gate_value = jnp.sum(hidden_grad * active * up_pre, axis=-1).astype(jnp.bfloat16)
    gate_part = (hidden_grad * up_pre * sigmoid * (1.0 + gate_pre * (1.0 - sigmoid))).astype(
        jnp.bfloat16
    )
    up_part = (hidden_grad * active).astype(jnp.bfloat16)
    input_back = lax.dot_general(
        gate_part, gate_matrix, (((1,), (1,)), ((), ())), preferred_element_type=jnp.float32
    ) + lax.dot_general(
        up_part, up_matrix, (((1,), (1,)), ((), ())), preferred_element_type=jnp.float32
    )
    return input_back.astype(jnp.bfloat16), gate_value


def expert_kernel(grad_ref, input_ref, gate_ref, up_ref, down_ref, back_ref, value_ref):
    grad_rows = grad_ref[...]
    input_rows = input_ref[...]
    gate_matrix = gate_ref[...]
    up_matrix = up_ref[...]
    gate_pre = jnp.dot(input_rows, gate_matrix, preferred_element_type=jnp.float32)
    up_pre = jnp.dot(input_rows, up_matrix, preferred_element_type=jnp.float32)
    hidden_grad = lax.dot_general(
        grad_rows, down_ref[...], (((1,), (1,)), ((), ())), preferred_element_type=jnp.float32
    )
    sigmoid = jax.nn.sigmoid(gate_pre)
    active = gate_pre * sigmoid
    value = jnp.sum(hidden_grad * active * up_pre, axis=-1, keepdims=True)
    value_ref[...] = jnp.broadcast_to(value, value_ref.shape)
    gate_part = (hidden_grad * up_pre * sigmoid * (1.0 + gate_pre * (1.0 - sigmoid))).astype(jnp.bfloat16)
    up_part = (hidden_grad * active).astype(jnp.bfloat16)
    back = lax.dot_general(
        gate_part, gate_matrix, (((1,), (1,)), ((), ())), preferred_element_type=jnp.float32
    ) + lax.dot_general(up_part, up_matrix, (((1,), (1,)), ((), ())), preferred_element_type=jnp.float32)
    back_ref[...] = back.astype(back_ref.dtype)

def expert_call(arrived, gate_matrix, up_matrix, down_matrix, tile=256):
    rows, both = arrived.shape
    width = both // 2
    hidden = gate_matrix.shape[1]
    steps = rows // tile
    flops = 2 * rows * width * hidden * 5
    cost = pl.CostEstimate(flops=flops, transcendentals=rows * hidden,
                           bytes_accessed=rows * both * 2 + 3 * width * hidden * 2 + rows * width * 2)
    back, value = pl.pallas_call(
        expert_kernel,
        grid=(steps,),
        in_specs=[
            pl.BlockSpec((tile, width), lambda i: (i, 0)),
            pl.BlockSpec((tile, width), lambda i: (i, 1)),
            pl.BlockSpec((width, hidden), lambda i: (0, 0)),
            pl.BlockSpec((width, hidden), lambda i: (0, 0)),
            pl.BlockSpec((hidden, width), lambda i: (0, 0)),
        ],
        out_specs=[
            pl.BlockSpec((tile, width), lambda i: (i, 0)),
            pl.BlockSpec((tile, 128), lambda i: (i, 0)),
        ],
        out_shape=[
            jax.ShapeDtypeStruct((rows, width), jnp.bfloat16),
            jax.ShapeDtypeStruct((rows, 128), jnp.float32),
        ],
        cost_estimate=cost,
    )(arrived, arrived, gate_matrix, up_matrix, down_matrix)
    return back, value[:, 0].astype(jnp.bfloat16)


def body(out_grad, layer_input, route_ids, route_probs, gate_weight, up_weight, down_weight):
    grad_tokens = out_grad[0]
    input_tokens = layer_input[0]
    chosen = route_ids[0]
    slot_probs = route_probs[0]
    gate_matrix = gate_weight[0, 0]
    up_matrix = up_weight[0, 0]
    down_matrix = down_weight[0, 0]
    peer_count = lax.axis_size("expert")
    token_count, top_count = chosen.shape
    model_width = grad_tokens.shape[1]
    capacity = min(token_count, 7 * token_count * top_count // (6 * peer_count))
    chunk = -(-(capacity + 1) // 16) * 8
    rows = peer_count * chunk

    flat_ids = chosen.reshape(-1)
    one_hot = (flat_ids[:, None] == jnp.arange(peer_count, dtype=jnp.int32)[None, :]).astype(
        jnp.int32
    )
    places = (jnp.sum(one_hot * jnp.cumsum(one_hot, axis=0), axis=1) - 1).reshape(
        token_count, top_count
    )
    ids = chosen
    lanes = jnp.arange(rows, dtype=jnp.int32)[None, None, :]
    both = jnp.concatenate([grad_tokens, input_tokens], axis=1)

    def dispatch(part):
        local = places - part * chunk
        inside = (local >= 0) & (local < chunk)
        target = jnp.where(inside, ids * chunk + local, -1)
        hits = target[:, :, None] == lanes
        pick = jnp.any(target[None, :, :] == lanes.reshape(rows, 1, 1), axis=2)
        weights = jnp.sum(jnp.where(hits, slot_probs[:, :, None], 0.0), axis=1)
        return pick, weights

    pick_a, weights_a = dispatch(0)
    send_a = jnp.dot(pick_a.astype(jnp.bfloat16), both, preferred_element_type=jnp.float32)
    send_a = send_a.astype(jnp.bfloat16).reshape(peer_count, chunk, 2 * model_width)
    unused, weights_b = dispatch(1)
    rest = capacity - chunk
    local = places - chunk
    grad_row = jnp.where(local >= 0, ids * 2 * rest + local, -1)
    input_row = jnp.where(local >= 0, grad_row + rest, -1)
    send_lanes = jnp.arange(peer_count * 2 * rest, dtype=jnp.int32).reshape(-1, 1, 1)
    pick_grad = jnp.any(grad_row[None, :, :] == send_lanes, axis=2).astype(jnp.bfloat16)
    pick_input = jnp.any(input_row[None, :, :] == send_lanes, axis=2).astype(jnp.bfloat16)
    send_b = jnp.dot(pick_grad, grad_tokens, preferred_element_type=jnp.float32) + jnp.dot(
        pick_input, input_tokens, preferred_element_type=jnp.float32
    )
    send_b = send_b.astype(jnp.bfloat16).reshape(peer_count, 2 * rest, model_width)

    arrived_a = lax.all_to_all(send_a, "expert", 0, 0, tiled=True).reshape(rows, 2 * model_width)
    arrived_b = lax.all_to_all(send_b, "expert", 0, 0, tiled=True)
    back_a, gate_a = expert_call(arrived_a, gate_matrix, up_matrix, down_matrix)
    back_a, gate_a, arrived_b = lax.optimization_barrier((back_a, gate_a, arrived_b))
    returned_a = lax.all_to_all(
        back_a.reshape(peer_count, chunk, model_width), "expert", 0, 0, tiled=True
    ).reshape(rows, model_width)
    arrived_b = (
        arrived_b.reshape(peer_count, 2, rest, model_width)
        .transpose(0, 2, 1, 3)
        .reshape(peer_count * rest, 2 * model_width)
    )
    back_b, gate_b = expert_call(arrived_b, gate_matrix, up_matrix, down_matrix, tile=192)
    gates = jnp.concatenate(
        [gate_a.reshape(peer_count, chunk), gate_b.reshape(peer_count, rest)], axis=1
    )
    gates = jnp.pad(gates, ((0, 0), (0, model_width - capacity)))
    back_b = jnp.concatenate(
        [
            back_b.reshape(peer_count, rest, model_width),
            gates[:, None, :],
            jnp.zeros((peer_count, chunk - rest - 1, model_width), back_b.dtype),
        ],
        axis=1,
    )
    returned_b = lax.all_to_all(back_b, "expert", 0, 0, tiled=True)
    gate_table = returned_b[:, rest, :capacity].reshape(-1)
    returned_b = returned_b.reshape(rows, model_width)

    def weighted(weights, returned):
        return jnp.dot(
            weights,
            returned.astype(jnp.float32),
            precision=lax.Precision.HIGHEST,
            preferred_element_type=jnp.float32,
        )

    combined = grad_tokens.astype(jnp.float32) + weighted(weights_a, returned_a)
    combined = combined + weighted(weights_b, returned_b)
    gate_index = ids * capacity + places
    gate_hits = gate_index[:, :, None] == jnp.arange(gate_table.shape[0], dtype=jnp.int32)
    gate_slot = jnp.sum(
        jnp.where(gate_hits, gate_table.astype(jnp.float32), 0.0), axis=2
    ).astype(jnp.bfloat16)
    passed = passed_along(combined.astype(jnp.bfloat16)[None], "pipe", -1)
    return (passed, gate_slot[None])


def solution(mesh):
    placed = (
        P("pipe", "expert", None),
        P("pipe", "expert", None),
        P("pipe", "expert", None),
        P("pipe", "expert", None),
        P("pipe", "expert", None, None),
        P("pipe", "expert", None, None),
        P("pipe", "expert", None, None),
    )
    return jax.shard_map(
        body,
        mesh=mesh,
        in_specs=placed,
        out_specs=(P("pipe", "expert", None), P("pipe", "expert", None)),
        check_vma=False,
    )
```

```python
import jax
import jax.numpy as jnp
from jax import lax
from jax.experimental import pallas as pl
from jax.sharding import PartitionSpec as P


def passed_along(value, axis, steps):
    count = lax.axis_size(axis)
    first, last = (max(0, -steps), min(count, count - steps))
    return lax.ppermute(value, axis, [(source, source + steps) for source in range(first, last)])


def expert_rows(grad_rows, input_rows, gate_matrix, up_matrix, down_matrix):
    gate_pre = jnp.dot(input_rows, gate_matrix, preferred_element_type=jnp.float32)
    up_pre = jnp.dot(input_rows, up_matrix, preferred_element_type=jnp.float32)
    hidden_grad = lax.dot_general(
        grad_rows, down_matrix, (((1,), (1,)), ((), ())), preferred_element_type=jnp.float32
    )
    sigmoid = jax.nn.sigmoid(gate_pre)
    active = gate_pre * sigmoid
    gate_value = jnp.sum(hidden_grad * active * up_pre, axis=-1).astype(jnp.bfloat16)
    gate_part = (hidden_grad * up_pre * sigmoid * (1.0 + gate_pre * (1.0 - sigmoid))).astype(
        jnp.bfloat16
    )
    up_part = (hidden_grad * active).astype(jnp.bfloat16)
    input_back = lax.dot_general(
        gate_part, gate_matrix, (((1,), (1,)), ((), ())), preferred_element_type=jnp.float32
    ) + lax.dot_general(
        up_part, up_matrix, (((1,), (1,)), ((), ())), preferred_element_type=jnp.float32
    )
    return input_back.astype(jnp.bfloat16), gate_value


def expert_kernel(grad_ref, input_ref, gate_ref, up_ref, down_ref, back_ref, value_ref):
    grad_rows = grad_ref[...]
    input_rows = input_ref[...]
    gate_matrix = gate_ref[...]
    up_matrix = up_ref[...]
    gate_pre = jnp.dot(input_rows, gate_matrix, preferred_element_type=jnp.float32)
    up_pre = jnp.dot(input_rows, up_matrix, preferred_element_type=jnp.float32)
    hidden_grad = lax.dot_general(
        grad_rows, down_ref[...], (((1,), (1,)), ((), ())), preferred_element_type=jnp.float32
    )
    sigmoid = jax.nn.sigmoid(gate_pre)
    active = gate_pre * sigmoid
    value = jnp.sum(hidden_grad * active * up_pre, axis=-1, keepdims=True)
    value_ref[...] = jnp.broadcast_to(value, value_ref.shape)
    gate_part = (hidden_grad * up_pre * sigmoid * (1.0 + gate_pre * (1.0 - sigmoid))).astype(jnp.bfloat16)
    up_part = (hidden_grad * active).astype(jnp.bfloat16)
    back = lax.dot_general(
        gate_part, gate_matrix, (((1,), (1,)), ((), ())), preferred_element_type=jnp.float32
    ) + lax.dot_general(up_part, up_matrix, (((1,), (1,)), ((), ())), preferred_element_type=jnp.float32)
    back_ref[...] = back.astype(back_ref.dtype)

def expert_call(arrived, gate_matrix, up_matrix, down_matrix, tile=256):
    rows, both = arrived.shape
    width = both // 2
    hidden = gate_matrix.shape[1]
    steps = rows // tile
    flops = 2 * rows * width * hidden * 5
    cost = pl.CostEstimate(flops=flops, transcendentals=rows * hidden,
                           bytes_accessed=rows * both * 2 + 3 * width * hidden * 2 + rows * width * 2)
    back, value = pl.pallas_call(
        expert_kernel,
        grid=(steps,),
        in_specs=[
            pl.BlockSpec((tile, width), lambda i: (i, 0)),
            pl.BlockSpec((tile, width), lambda i: (i, 1)),
            pl.BlockSpec((width, hidden), lambda i: (0, 0)),
            pl.BlockSpec((width, hidden), lambda i: (0, 0)),
            pl.BlockSpec((hidden, width), lambda i: (0, 0)),
        ],
        out_specs=[
            pl.BlockSpec((tile, width), lambda i: (i, 0)),
            pl.BlockSpec((tile, 128), lambda i: (i, 0)),
        ],
        out_shape=[
            jax.ShapeDtypeStruct((rows, width), jnp.bfloat16),
            jax.ShapeDtypeStruct((rows, 128), jnp.float32),
        ],
        cost_estimate=cost,
    )(arrived, arrived, gate_matrix, up_matrix, down_matrix)
    return back, value[:, 0].astype(jnp.bfloat16)


def pick_kernel(pick_ref, rows_ref, out_ref):
    out_ref[...] = jnp.dot(
        pick_ref[...], rows_ref[...], preferred_element_type=jnp.float32
    ).astype(out_ref.dtype)


def pick_rows(pick, table, block=1280):
    count, width = pick.shape[0], table.shape[1]
    return pl.pallas_call(
        pick_kernel,
        grid=(width // block,),
        in_specs=[
            pl.BlockSpec(pick.shape, lambda j: (0, 0)),
            pl.BlockSpec((table.shape[0], block), lambda j: (0, j)),
        ],
        out_specs=pl.BlockSpec((count, block), lambda j: (0, j)),
        out_shape=jax.ShapeDtypeStruct((count, width), table.dtype),
        cost_estimate=pl.CostEstimate(
            flops=2 * count * table.shape[0] * width,
            transcendentals=0,
            bytes_accessed=2 * (count * table.shape[0] + table.size + count * width),
        ),
    )(pick, table)


def body(out_grad, layer_input, route_ids, route_probs, gate_weight, up_weight, down_weight):
    grad_tokens = out_grad[0]
    input_tokens = layer_input[0]
    chosen = route_ids[0]
    slot_probs = route_probs[0]
    gate_matrix = gate_weight[0, 0]
    up_matrix = up_weight[0, 0]
    down_matrix = down_weight[0, 0]
    peer_count = lax.axis_size("expert")
    token_count, top_count = chosen.shape
    model_width = grad_tokens.shape[1]
    capacity = min(token_count, 7 * token_count * top_count // (6 * peer_count))
    chunk = -(-(capacity + 1) // 16) * 8
    rows = peer_count * chunk

    flat_ids = chosen.reshape(-1)
    one_hot = (flat_ids[:, None] == jnp.arange(peer_count, dtype=jnp.int32)[None, :]).astype(
        jnp.int32
    )
    places = (jnp.sum(one_hot * jnp.cumsum(one_hot, axis=0), axis=1) - 1).reshape(
        token_count, top_count
    )
    ids = chosen
    lanes = jnp.arange(rows, dtype=jnp.int32)[None, None, :]
    both = jnp.concatenate([grad_tokens, input_tokens], axis=1)

    def dispatch(part):
        local = places - part * chunk
        inside = (local >= 0) & (local < chunk)
        target = jnp.where(inside, ids * chunk + local, -1)
        hits = target[:, :, None] == lanes
        pick = jnp.any(target[None, :, :] == lanes.reshape(rows, 1, 1), axis=2)
        weights = jnp.sum(jnp.where(hits, slot_probs[:, :, None], 0.0), axis=1)
        return pick, weights

    pick_a, weights_a = dispatch(0)
    send_a = pick_rows(pick_a.astype(jnp.bfloat16), both)
    send_a = send_a.reshape(peer_count, chunk, 2 * model_width)
    unused, weights_b = dispatch(1)
    rest = capacity - chunk
    local = places - chunk
    grad_row = jnp.where(local >= 0, ids * 2 * rest + local, -1)
    input_row = jnp.where(local >= 0, grad_row + rest, -1)
    send_lanes = jnp.arange(peer_count * 2 * rest, dtype=jnp.int32).reshape(-1, 1, 1)
    pick_grad = jnp.any(grad_row[None, :, :] == send_lanes, axis=2).astype(jnp.bfloat16)
    pick_input = jnp.any(input_row[None, :, :] == send_lanes, axis=2).astype(jnp.bfloat16)
    send_b = jnp.dot(pick_grad, grad_tokens, preferred_element_type=jnp.float32) + jnp.dot(
        pick_input, input_tokens, preferred_element_type=jnp.float32
    )
    send_b = send_b.astype(jnp.bfloat16).reshape(peer_count, 2 * rest, model_width)

    arrived_a = lax.all_to_all(send_a, "expert", 0, 0, tiled=True).reshape(rows, 2 * model_width)
    arrived_b = lax.all_to_all(send_b, "expert", 0, 0, tiled=True)
    back_a, gate_a = expert_call(arrived_a, gate_matrix, up_matrix, down_matrix)
    back_a, gate_a, arrived_b = lax.optimization_barrier((back_a, gate_a, arrived_b))
    returned_a = lax.all_to_all(
        back_a.reshape(peer_count, chunk, model_width), "expert", 0, 0, tiled=True
    ).reshape(rows, model_width)
    arrived_b = (
        arrived_b.reshape(peer_count, 2, rest, model_width)
        .transpose(0, 2, 1, 3)
        .reshape(peer_count * rest, 2 * model_width)
    )
    back_b, gate_b = expert_call(arrived_b, gate_matrix, up_matrix, down_matrix, tile=192)
    gates = jnp.concatenate(
        [gate_a.reshape(peer_count, chunk), gate_b.reshape(peer_count, rest)], axis=1
    )
    gates = jnp.pad(gates, ((0, 0), (0, model_width - capacity)))
    back_b = jnp.concatenate(
        [
            back_b.reshape(peer_count, rest, model_width),
            gates[:, None, :],
            jnp.zeros((peer_count, chunk - rest - 1, model_width), back_b.dtype),
        ],
        axis=1,
    )
    returned_b = lax.all_to_all(back_b, "expert", 0, 0, tiled=True)
    gate_table = returned_b[:, rest, :capacity].reshape(-1)
    returned_b = returned_b.reshape(rows, model_width)

    def weighted(weights, returned):
        return jnp.dot(
            weights,
            returned.astype(jnp.float32),
            precision=lax.Precision.HIGHEST,
            preferred_element_type=jnp.float32,
        )

    combined = grad_tokens.astype(jnp.float32) + weighted(weights_a, returned_a)
    combined = combined + weighted(weights_b, returned_b)
    gate_index = ids * capacity + places
    gate_hits = gate_index[:, :, None] == jnp.arange(gate_table.shape[0], dtype=jnp.int32)
    gate_slot = jnp.sum(
        jnp.where(gate_hits, gate_table.astype(jnp.float32), 0.0), axis=2
    ).astype(jnp.bfloat16)
    passed = passed_along(combined.astype(jnp.bfloat16)[None], "pipe", -1)
    return (passed, gate_slot[None])


def solution(mesh):
    placed = (
        P("pipe", "expert", None),
        P("pipe", "expert", None),
        P("pipe", "expert", None),
        P("pipe", "expert", None),
        P("pipe", "expert", None, None),
        P("pipe", "expert", None, None),
        P("pipe", "expert", None, None),
    )
    return jax.shard_map(
        body,
        mesh=mesh,
        in_specs=placed,
        out_specs=(P("pipe", "expert", None), P("pipe", "expert", None)),
        check_vma=False,
    )
```

```python
import jax
import jax.numpy as jnp
from jax import lax
from jax.experimental import pallas as pl
from jax.sharding import PartitionSpec as P


def passed_along(value, axis, steps):
    count = lax.axis_size(axis)
    first, last = (max(0, -steps), min(count, count - steps))
    return lax.ppermute(value, axis, [(source, source + steps) for source in range(first, last)])


def expert_rows(grad_rows, input_rows, gate_matrix, up_matrix, down_matrix):
    gate_pre = jnp.dot(input_rows, gate_matrix, preferred_element_type=jnp.float32)
    up_pre = jnp.dot(input_rows, up_matrix, preferred_element_type=jnp.float32)
    hidden_grad = lax.dot_general(
        grad_rows, down_matrix, (((1,), (1,)), ((), ())), preferred_element_type=jnp.float32
    )
    sigmoid = jax.nn.sigmoid(gate_pre)
    active = gate_pre * sigmoid
    gate_value = jnp.sum(hidden_grad * active * up_pre, axis=-1).astype(jnp.bfloat16)
    gate_part = (hidden_grad * up_pre * sigmoid * (1.0 + gate_pre * (1.0 - sigmoid))).astype(
        jnp.bfloat16
    )
    up_part = (hidden_grad * active).astype(jnp.bfloat16)
    input_back = lax.dot_general(
        gate_part, gate_matrix, (((1,), (1,)), ((), ())), preferred_element_type=jnp.float32
    ) + lax.dot_general(
        up_part, up_matrix, (((1,), (1,)), ((), ())), preferred_element_type=jnp.float32
    )
    return input_back.astype(jnp.bfloat16), gate_value


def expert_kernel(grad_ref, input_ref, gate_ref, up_ref, down_ref, back_ref, value_ref):
    grad_rows = grad_ref[...]
    input_rows = input_ref[...]
    gate_matrix = gate_ref[...]
    up_matrix = up_ref[...]
    gate_pre = jnp.dot(input_rows, gate_matrix, preferred_element_type=jnp.float32)
    up_pre = jnp.dot(input_rows, up_matrix, preferred_element_type=jnp.float32)
    hidden_grad = lax.dot_general(
        grad_rows, down_ref[...], (((1,), (1,)), ((), ())), preferred_element_type=jnp.float32
    )
    sigmoid = jax.nn.sigmoid(gate_pre)
    active = gate_pre * sigmoid
    value = jnp.sum(hidden_grad * active * up_pre, axis=-1, keepdims=True)
    value_ref[...] = jnp.broadcast_to(value, value_ref.shape)
    gate_part = (hidden_grad * up_pre * sigmoid * (1.0 + gate_pre * (1.0 - sigmoid))).astype(jnp.bfloat16)
    up_part = (hidden_grad * active).astype(jnp.bfloat16)
    back = lax.dot_general(
        gate_part, gate_matrix, (((1,), (1,)), ((), ())), preferred_element_type=jnp.float32
    ) + lax.dot_general(up_part, up_matrix, (((1,), (1,)), ((), ())), preferred_element_type=jnp.float32)
    back_ref[...] = back.astype(back_ref.dtype)

def expert_call(arrived, gate_matrix, up_matrix, down_matrix, tile=256):
    rows, both = arrived.shape
    width = both // 2
    hidden = gate_matrix.shape[1]
    steps = rows // tile
    flops = 2 * rows * width * hidden * 5
    cost = pl.CostEstimate(flops=flops, transcendentals=rows * hidden,
                           bytes_accessed=rows * both * 2 + 3 * width * hidden * 2 + rows * width * 2)
    back, value = pl.pallas_call(
        expert_kernel,
        grid=(steps,),
        in_specs=[
            pl.BlockSpec((tile, width), lambda i: (i, 0)),
            pl.BlockSpec((tile, width), lambda i: (i, 1)),
            pl.BlockSpec((width, hidden), lambda i: (0, 0)),
            pl.BlockSpec((width, hidden), lambda i: (0, 0)),
            pl.BlockSpec((hidden, width), lambda i: (0, 0)),
        ],
        out_specs=[
            pl.BlockSpec((tile, width), lambda i: (i, 0)),
            pl.BlockSpec((tile, 128), lambda i: (i, 0)),
        ],
        out_shape=[
            jax.ShapeDtypeStruct((rows, width), jnp.bfloat16),
            jax.ShapeDtypeStruct((rows, 128), jnp.float32),
        ],
        cost_estimate=cost,
    )(arrived, arrived, gate_matrix, up_matrix, down_matrix)
    return back, value[:, 0].astype(jnp.bfloat16)


def body(out_grad, layer_input, route_ids, route_probs, gate_weight, up_weight, down_weight):
    grad_tokens = out_grad[0]
    input_tokens = layer_input[0]
    chosen = route_ids[0]
    slot_probs = route_probs[0]
    gate_matrix = gate_weight[0, 0]
    up_matrix = up_weight[0, 0]
    down_matrix = down_weight[0, 0]
    peer_count = lax.axis_size("expert")
    token_count, top_count = chosen.shape
    model_width = grad_tokens.shape[1]
    capacity = min(token_count, 7 * token_count * top_count // (6 * peer_count))
    chunk = -(-(capacity + 1) // 16) * 8
    rows = peer_count * chunk

    named = chosen[:, :, None] == jnp.arange(peer_count, dtype=jnp.int32)[None, None, :]
    incidence = jnp.any(named, axis=1).astype(jnp.bfloat16)
    token_iota = jnp.arange(token_count, dtype=jnp.int32)
    earlier = (token_iota[None, :] < token_iota[:, None]).astype(jnp.bfloat16)
    before = jnp.dot(earlier, incidence, preferred_element_type=jnp.float32)
    places = jnp.sum(jnp.where(named, before[:, None, :], 0.0), axis=2).astype(jnp.int32)
    ids = chosen
    lanes = jnp.arange(rows, dtype=jnp.int32)[None, None, :]
    both = jnp.concatenate([grad_tokens, input_tokens], axis=1)

    def dispatch(part):
        local = places - part * chunk
        inside = (local >= 0) & (local < chunk)
        target = jnp.where(inside, ids * chunk + local, -1)
        hits = target[:, :, None] == lanes
        pick = jnp.any(target[None, :, :] == lanes.reshape(rows, 1, 1), axis=2)
        weights = jnp.sum(jnp.where(hits, slot_probs[:, :, None], 0.0), axis=1)
        return pick, weights

    pick_a, weights_a = dispatch(0)
    send_a = jnp.dot(pick_a.astype(jnp.bfloat16), both, preferred_element_type=jnp.float32)
    send_a = send_a.astype(jnp.bfloat16).reshape(peer_count, chunk, 2 * model_width)
    unused, weights_b = dispatch(1)
    rest = capacity - chunk
    local = places - chunk
    grad_row = jnp.where(local >= 0, ids * 2 * rest + local, -1)
    input_row = jnp.where(local >= 0, grad_row + rest, -1)
    send_lanes = jnp.arange(peer_count * 2 * rest, dtype=jnp.int32).reshape(-1, 1, 1)
    pick_grad = jnp.any(grad_row[None, :, :] == send_lanes, axis=2).astype(jnp.bfloat16)
    pick_input = jnp.any(input_row[None, :, :] == send_lanes, axis=2).astype(jnp.bfloat16)
    send_b = jnp.dot(pick_grad, grad_tokens, preferred_element_type=jnp.float32) + jnp.dot(
        pick_input, input_tokens, preferred_element_type=jnp.float32
    )
    send_b = send_b.astype(jnp.bfloat16).reshape(peer_count, 2 * rest, model_width)

    arrived_a = lax.all_to_all(send_a, "expert", 0, 0, tiled=True).reshape(rows, 2 * model_width)
    arrived_b = lax.all_to_all(send_b, "expert", 0, 0, tiled=True)
    back_a, gate_a = expert_call(arrived_a, gate_matrix, up_matrix, down_matrix)
    back_a, gate_a, arrived_b = lax.optimization_barrier((back_a, gate_a, arrived_b))
    returned_a = lax.all_to_all(
        back_a.reshape(peer_count, chunk, model_width), "expert", 0, 0, tiled=True
    ).reshape(rows, model_width)
    arrived_b = (
        arrived_b.reshape(peer_count, 2, rest, model_width)
        .transpose(0, 2, 1, 3)
        .reshape(peer_count * rest, 2 * model_width)
    )
    back_b, gate_b = expert_call(arrived_b, gate_matrix, up_matrix, down_matrix, tile=192)
    gates = jnp.concatenate(
        [gate_a.reshape(peer_count, chunk), gate_b.reshape(peer_count, rest)], axis=1
    )
    gates = jnp.pad(gates, ((0, 0), (0, model_width - capacity)))
    back_b = jnp.concatenate(
        [
            back_b.reshape(peer_count, rest, model_width),
            gates[:, None, :],
            jnp.zeros((peer_count, chunk - rest - 1, model_width), back_b.dtype),
        ],
        axis=1,
    )
    returned_b = lax.all_to_all(back_b, "expert", 0, 0, tiled=True)
    gate_table = returned_b[:, rest, :capacity].reshape(-1)
    returned_b = returned_b.reshape(rows, model_width)

    def weighted(weights, returned):
        return jnp.dot(
            weights,
            returned.astype(jnp.float32),
            precision=lax.Precision.HIGHEST,
            preferred_element_type=jnp.float32,
        )

    combined = grad_tokens.astype(jnp.float32) + weighted(weights_a, returned_a)
    combined = combined + weighted(weights_b, returned_b)
    gate_index = ids * capacity + places
    gate_hits = gate_index[:, :, None] == jnp.arange(gate_table.shape[0], dtype=jnp.int32)
    gate_slot = jnp.sum(
        jnp.where(gate_hits, gate_table.astype(jnp.float32), 0.0), axis=2
    ).astype(jnp.bfloat16)
    passed = passed_along(combined.astype(jnp.bfloat16)[None], "pipe", -1)
    return (passed, gate_slot[None])


def solution(mesh):
    placed = (
        P("pipe", "expert", None),
        P("pipe", "expert", None),
        P("pipe", "expert", None),
        P("pipe", "expert", None),
        P("pipe", "expert", None, None),
        P("pipe", "expert", None, None),
        P("pipe", "expert", None, None),
    )
    return jax.shard_map(
        body,
        mesh=mesh,
        in_specs=placed,
        out_specs=(P("pipe", "expert", None), P("pipe", "expert", None)),
        check_vma=False,
    )
```

```python
import jax
import jax.numpy as jnp
from jax import lax
from jax.experimental import pallas as pl
from jax.sharding import PartitionSpec as P


def passed_along(value, axis, steps):
    count = lax.axis_size(axis)
    first, last = (max(0, -steps), min(count, count - steps))
    return lax.ppermute(value, axis, [(source, source + steps) for source in range(first, last)])


def expert_rows(grad_rows, input_rows, gate_matrix, up_matrix, down_matrix):
    gate_pre = jnp.dot(input_rows, gate_matrix, preferred_element_type=jnp.float32)
    up_pre = jnp.dot(input_rows, up_matrix, preferred_element_type=jnp.float32)
    hidden_grad = lax.dot_general(
        grad_rows, down_matrix, (((1,), (1,)), ((), ())), preferred_element_type=jnp.float32
    )
    sigmoid = jax.nn.sigmoid(gate_pre)
    active = gate_pre * sigmoid
    gate_value = jnp.sum(hidden_grad * active * up_pre, axis=-1).astype(jnp.bfloat16)
    gate_part = (hidden_grad * up_pre * sigmoid * (1.0 + gate_pre * (1.0 - sigmoid))).astype(
        jnp.bfloat16
    )
    up_part = (hidden_grad * active).astype(jnp.bfloat16)
    input_back = lax.dot_general(
        gate_part, gate_matrix, (((1,), (1,)), ((), ())), preferred_element_type=jnp.float32
    ) + lax.dot_general(
        up_part, up_matrix, (((1,), (1,)), ((), ())), preferred_element_type=jnp.float32
    )
    return input_back.astype(jnp.bfloat16), gate_value


def expert_kernel(grad_ref, input_ref, gate_ref, up_ref, down_ref, back_ref, value_ref):
    grad_rows = grad_ref[...]
    input_rows = input_ref[...]
    gate_matrix = gate_ref[...]
    up_matrix = up_ref[...]
    gate_pre = jnp.dot(input_rows, gate_matrix, preferred_element_type=jnp.float32)
    up_pre = jnp.dot(input_rows, up_matrix, preferred_element_type=jnp.float32)
    hidden_grad = lax.dot_general(
        grad_rows, down_ref[...], (((1,), (1,)), ((), ())), preferred_element_type=jnp.float32
    )
    sigmoid = jax.nn.sigmoid(gate_pre)
    active = gate_pre * sigmoid
    value = jnp.sum(hidden_grad * active * up_pre, axis=-1, keepdims=True)
    value_ref[...] = jnp.broadcast_to(value, value_ref.shape)
    gate_part = (hidden_grad * up_pre * sigmoid * (1.0 + gate_pre * (1.0 - sigmoid))).astype(jnp.bfloat16)
    up_part = (hidden_grad * active).astype(jnp.bfloat16)
    back = lax.dot_general(
        gate_part, gate_matrix, (((1,), (1,)), ((), ())), preferred_element_type=jnp.float32
    ) + lax.dot_general(up_part, up_matrix, (((1,), (1,)), ((), ())), preferred_element_type=jnp.float32)
    back_ref[...] = back.astype(back_ref.dtype)

def expert_call(arrived, gate_matrix, up_matrix, down_matrix, tile=256):
    rows, both = arrived.shape
    width = both // 2
    hidden = gate_matrix.shape[1]
    steps = rows // tile
    flops = 2 * rows * width * hidden * 5
    cost = pl.CostEstimate(flops=flops, transcendentals=rows * hidden,
                           bytes_accessed=rows * both * 2 + 3 * width * hidden * 2 + rows * width * 2)
    back, value = pl.pallas_call(
        expert_kernel,
        grid=(steps,),
        in_specs=[
            pl.BlockSpec((tile, width), lambda i: (i, 0)),
            pl.BlockSpec((tile, width), lambda i: (i, 1)),
            pl.BlockSpec((width, hidden), lambda i: (0, 0)),
            pl.BlockSpec((width, hidden), lambda i: (0, 0)),
            pl.BlockSpec((hidden, width), lambda i: (0, 0)),
        ],
        out_specs=[
            pl.BlockSpec((tile, width), lambda i: (i, 0)),
            pl.BlockSpec((tile, 128), lambda i: (i, 0)),
        ],
        out_shape=[
            jax.ShapeDtypeStruct((rows, width), jnp.bfloat16),
            jax.ShapeDtypeStruct((rows, 128), jnp.float32),
        ],
        cost_estimate=cost,
    )(arrived, arrived, gate_matrix, up_matrix, down_matrix)
    return back, value[:, 0].astype(jnp.bfloat16)


def body(out_grad, layer_input, route_ids, route_probs, gate_weight, up_weight, down_weight):
    grad_tokens = out_grad[0]
    input_tokens = layer_input[0]
    chosen = route_ids[0]
    slot_probs = route_probs[0]
    gate_matrix = gate_weight[0, 0]
    up_matrix = up_weight[0, 0]
    down_matrix = down_weight[0, 0]
    peer_count = lax.axis_size("expert")
    token_count, top_count = chosen.shape
    model_width = grad_tokens.shape[1]
    capacity = min(token_count, 7 * token_count * top_count // (6 * peer_count))
    chunk = -(-(capacity + 1) // 16) * 8
    rows = peer_count * chunk

    named = chosen[:, :, None] == jnp.arange(peer_count, dtype=jnp.int32)[None, None, :]
    incidence = jnp.any(named, axis=1).astype(jnp.bfloat16)
    token_iota = jnp.arange(token_count, dtype=jnp.int32)
    earlier = (token_iota[None, :] < token_iota[:, None]).astype(jnp.bfloat16)
    before = jnp.dot(earlier, incidence, preferred_element_type=jnp.float32)
    places = jnp.sum(jnp.where(named, before[:, None, :], 0.0), axis=2).astype(jnp.int32)
    ids = chosen
    lanes = jnp.arange(rows, dtype=jnp.int32)[None, None, :]
    both = jnp.concatenate([grad_tokens, input_tokens], axis=1)

    def dispatch(part):
        local = places - part * chunk
        inside = (local >= 0) & (local < chunk)
        target = jnp.where(inside, ids * chunk + local, -1)
        hits = target[:, :, None] == lanes
        pick = jnp.any(target[None, :, :] == lanes.reshape(rows, 1, 1), axis=2)
        weights = jnp.sum(jnp.where(hits, slot_probs[:, :, None], 0.0), axis=1)
        return pick, weights

    pick_a, weights_a = dispatch(0)
    send_a = jnp.dot(pick_a.astype(jnp.bfloat16), both, preferred_element_type=jnp.float32)
    send_a = send_a.astype(jnp.bfloat16).reshape(peer_count, chunk, 2 * model_width)
    unused, weights_b = dispatch(1)
    rest = capacity - chunk
    local = places - chunk
    grad_row = jnp.where(local >= 0, ids * 2 * rest + local, -1)
    input_row = jnp.where(local >= 0, grad_row + rest, -1)
    send_lanes = jnp.arange(peer_count * 2 * rest, dtype=jnp.int32).reshape(-1, 1, 1)
    pick_grad = jnp.any(grad_row[None, :, :] == send_lanes, axis=2).astype(jnp.bfloat16)
    pick_input = jnp.any(input_row[None, :, :] == send_lanes, axis=2).astype(jnp.bfloat16)
    send_b = jnp.dot(pick_grad, grad_tokens, preferred_element_type=jnp.float32) + jnp.dot(
        pick_input, input_tokens, preferred_element_type=jnp.float32
    )
    send_b = send_b.astype(jnp.bfloat16).reshape(peer_count, 2 * rest, model_width)

    arrived_a = lax.all_to_all(send_a, "expert", 0, 0, tiled=True).reshape(rows, 2 * model_width)
    arrived_b = lax.all_to_all(send_b, "expert", 0, 0, tiled=True)
    back_a, gate_a = expert_call(arrived_a, gate_matrix, up_matrix, down_matrix)
    back_a, gate_a, arrived_b = lax.optimization_barrier((back_a, gate_a, arrived_b))
    returned_a = lax.all_to_all(
        back_a.reshape(peer_count, chunk, model_width), "expert", 0, 0, tiled=True
    ).reshape(rows, model_width)
    arrived_b = (
        arrived_b.reshape(peer_count, 2, rest, model_width)
        .transpose(0, 2, 1, 3)
        .reshape(peer_count * rest, 2 * model_width)
    )
    back_b, gate_b = expert_call(arrived_b, gate_matrix, up_matrix, down_matrix, tile=192)
    gates = jnp.concatenate(
        [gate_a.reshape(peer_count, chunk), gate_b.reshape(peer_count, rest)], axis=1
    )
    gates = jnp.pad(gates, ((0, 0), (0, model_width - capacity)))
    back_b = jnp.concatenate(
        [
            back_b.reshape(peer_count, rest, model_width),
            gates[:, None, :],
            jnp.zeros((peer_count, chunk - rest - 1, model_width), back_b.dtype),
        ],
        axis=1,
    )
    returned_b = lax.all_to_all(back_b, "expert", 0, 0, tiled=True)
    gate_table = returned_b[:, rest, :capacity].reshape(-1)
    returned_b = returned_b.reshape(rows, model_width)

    def weighted(weights, returned):
        return jnp.dot(
            weights,
            returned.astype(jnp.float32),
            precision=lax.Precision.HIGHEST,
            preferred_element_type=jnp.float32,
        )

    combined = grad_tokens.astype(jnp.float32) + weighted(weights_a, returned_a)
    combined = combined + jnp.dot(
        weights_b,
        returned_b.astype(jnp.float32),
        precision=lax.Precision.HIGH,
        preferred_element_type=jnp.float32,
    )
    gate_index = ids * capacity + places
    gate_hits = gate_index[:, :, None] == jnp.arange(gate_table.shape[0], dtype=jnp.int32)
    gate_slot = jnp.sum(
        jnp.where(gate_hits, gate_table.astype(jnp.float32), 0.0), axis=2
    ).astype(jnp.bfloat16)
    passed = passed_along(combined.astype(jnp.bfloat16)[None], "pipe", -1)
    return (passed, gate_slot[None])


def solution(mesh):
    placed = (
        P("pipe", "expert", None),
        P("pipe", "expert", None),
        P("pipe", "expert", None),
        P("pipe", "expert", None),
        P("pipe", "expert", None, None),
        P("pipe", "expert", None, None),
        P("pipe", "expert", None, None),
    )
    return jax.shard_map(
        body,
        mesh=mesh,
        in_specs=placed,
        out_specs=(P("pipe", "expert", None), P("pipe", "expert", None)),
        check_vma=False,
    )
```

```python
import jax
import jax.numpy as jnp
from jax import lax
from jax.experimental import pallas as pl
from jax.sharding import PartitionSpec as P


def passed_along(value, axis, steps):
    count = lax.axis_size(axis)
    first, last = (max(0, -steps), min(count, count - steps))
    return lax.ppermute(value, axis, [(source, source + steps) for source in range(first, last)])


def expert_rows(grad_rows, input_rows, gate_matrix, up_matrix, down_matrix):
    gate_pre = jnp.dot(input_rows, gate_matrix, preferred_element_type=jnp.float32)
    up_pre = jnp.dot(input_rows, up_matrix, preferred_element_type=jnp.float32)
    hidden_grad = lax.dot_general(
        grad_rows, down_matrix, (((1,), (1,)), ((), ())), preferred_element_type=jnp.float32
    )
    sigmoid = jax.nn.sigmoid(gate_pre)
    active = gate_pre * sigmoid
    gate_value = jnp.sum(hidden_grad * active * up_pre, axis=-1).astype(jnp.bfloat16)
    gate_part = (hidden_grad * up_pre * sigmoid * (1.0 + gate_pre * (1.0 - sigmoid))).astype(
        jnp.bfloat16
    )
    up_part = (hidden_grad * active).astype(jnp.bfloat16)
    input_back = lax.dot_general(
        gate_part, gate_matrix, (((1,), (1,)), ((), ())), preferred_element_type=jnp.float32
    ) + lax.dot_general(
        up_part, up_matrix, (((1,), (1,)), ((), ())), preferred_element_type=jnp.float32
    )
    return input_back.astype(jnp.bfloat16), gate_value


def expert_kernel(grad_ref, input_ref, gate_ref, up_ref, down_ref, back_ref, value_ref):
    grad_rows = grad_ref[...]
    input_rows = input_ref[...]
    gate_matrix = gate_ref[...]
    up_matrix = up_ref[...]
    gate_pre = jnp.dot(input_rows, gate_matrix, preferred_element_type=jnp.float32)
    up_pre = jnp.dot(input_rows, up_matrix, preferred_element_type=jnp.float32)
    hidden_grad = lax.dot_general(
        grad_rows, down_ref[...], (((1,), (1,)), ((), ())), preferred_element_type=jnp.float32
    )
    sigmoid = jax.nn.sigmoid(gate_pre)
    active = gate_pre * sigmoid
    value = jnp.sum(hidden_grad * active * up_pre, axis=-1, keepdims=True)
    value_ref[...] = jnp.broadcast_to(value, value_ref.shape)
    gate_part = (hidden_grad * up_pre * sigmoid * (1.0 + gate_pre * (1.0 - sigmoid))).astype(jnp.bfloat16)
    up_part = (hidden_grad * active).astype(jnp.bfloat16)
    back = lax.dot_general(
        gate_part, gate_matrix, (((1,), (1,)), ((), ())), preferred_element_type=jnp.float32
    ) + lax.dot_general(up_part, up_matrix, (((1,), (1,)), ((), ())), preferred_element_type=jnp.float32)
    back_ref[...] = back.astype(back_ref.dtype)

def expert_call(arrived, gate_matrix, up_matrix, down_matrix, tile=256):
    rows, both = arrived.shape
    width = both // 2
    hidden = gate_matrix.shape[1]
    steps = rows // tile
    flops = 2 * rows * width * hidden * 5
    cost = pl.CostEstimate(flops=flops, transcendentals=rows * hidden,
                           bytes_accessed=rows * both * 2 + 3 * width * hidden * 2 + rows * width * 2)
    back, value = pl.pallas_call(
        expert_kernel,
        grid=(steps,),
        in_specs=[
            pl.BlockSpec((tile, width), lambda i: (i, 0)),
            pl.BlockSpec((tile, width), lambda i: (i, 1)),
            pl.BlockSpec((width, hidden), lambda i: (0, 0)),
            pl.BlockSpec((width, hidden), lambda i: (0, 0)),
            pl.BlockSpec((hidden, width), lambda i: (0, 0)),
        ],
        out_specs=[
            pl.BlockSpec((tile, width), lambda i: (i, 0)),
            pl.BlockSpec((tile, 128), lambda i: (i, 0)),
        ],
        out_shape=[
            jax.ShapeDtypeStruct((rows, width), jnp.bfloat16),
            jax.ShapeDtypeStruct((rows, 128), jnp.float32),
        ],
        cost_estimate=cost,
    )(arrived, arrived, gate_matrix, up_matrix, down_matrix)
    return back, value[:, 0].astype(jnp.bfloat16)


def body(out_grad, layer_input, route_ids, route_probs, gate_weight, up_weight, down_weight):
    grad_tokens = out_grad[0]
    input_tokens = layer_input[0]
    chosen = route_ids[0]
    slot_probs = route_probs[0]
    gate_matrix = gate_weight[0, 0]
    up_matrix = up_weight[0, 0]
    down_matrix = down_weight[0, 0]
    peer_count = lax.axis_size("expert")
    token_count, top_count = chosen.shape
    model_width = grad_tokens.shape[1]
    capacity = min(token_count, 7 * token_count * top_count // (6 * peer_count))
    chunk = (capacity - 1) // 8 * 8
    tail = -(-(capacity - chunk + 1) // 8) * 8
    rows = peer_count * chunk

    named = chosen[:, :, None] == jnp.arange(peer_count, dtype=jnp.int32)[None, None, :]
    incidence = jnp.any(named, axis=1).astype(jnp.bfloat16)
    token_iota = jnp.arange(token_count, dtype=jnp.int32)
    earlier = (token_iota[None, :] < token_iota[:, None]).astype(jnp.bfloat16)
    before = jnp.dot(earlier, incidence, preferred_element_type=jnp.float32)
    places = jnp.sum(jnp.where(named, before[:, None, :], 0.0), axis=2).astype(jnp.int32)
    ids = chosen
    both = jnp.concatenate([grad_tokens, input_tokens], axis=1)

    def dispatch(offset, block):
        local = places - offset
        inside = (local >= 0) & (local < block)
        target = jnp.where(inside, ids * block + local, -1)
        lanes = jnp.arange(peer_count * block, dtype=jnp.int32)
        hits = target[:, :, None] == lanes[None, None, :]
        pick = jnp.any(target[None, :, :] == lanes[:, None, None], axis=2)
        weights = jnp.sum(jnp.where(hits, slot_probs[:, :, None], 0.0), axis=1)
        return pick, weights

    pick_a, weights_a = dispatch(0, chunk)
    send_a = jnp.dot(pick_a.astype(jnp.bfloat16), both, preferred_element_type=jnp.float32)
    send_a = send_a.astype(jnp.bfloat16).reshape(peer_count, chunk, 2 * model_width)
    unused, weights_b = dispatch(chunk, tail)
    rest = capacity - chunk
    local = places - chunk
    grad_row = jnp.where(local >= 0, ids * 2 * rest + local, -1)
    input_row = jnp.where(local >= 0, grad_row + rest, -1)
    send_lanes = jnp.arange(peer_count * 2 * rest, dtype=jnp.int32).reshape(-1, 1, 1)
    pick_grad = jnp.any(grad_row[None, :, :] == send_lanes, axis=2).astype(jnp.bfloat16)
    pick_input = jnp.any(input_row[None, :, :] == send_lanes, axis=2).astype(jnp.bfloat16)
    send_b = jnp.dot(pick_grad, grad_tokens, preferred_element_type=jnp.float32) + jnp.dot(
        pick_input, input_tokens, preferred_element_type=jnp.float32
    )
    send_b = send_b.astype(jnp.bfloat16).reshape(peer_count, 2 * rest, model_width)

    arrived_a = lax.all_to_all(send_a, "expert", 0, 0, tiled=True).reshape(rows, 2 * model_width)
    arrived_b = lax.all_to_all(send_b, "expert", 0, 0, tiled=True)
    back_a, gate_a = expert_call(arrived_a, gate_matrix, up_matrix, down_matrix)
    back_a, gate_a, arrived_b = lax.optimization_barrier((back_a, gate_a, arrived_b))
    returned_a = lax.all_to_all(
        back_a.reshape(peer_count, chunk, model_width), "expert", 0, 0, tiled=True
    ).reshape(rows, model_width)
    arrived_b = (
        arrived_b.reshape(peer_count, 2, rest, model_width)
        .transpose(0, 2, 1, 3)
        .reshape(peer_count * rest, 2 * model_width)
    )
    back_b, gate_b = expert_call(arrived_b, gate_matrix, up_matrix, down_matrix, tile=128)
    gates = jnp.concatenate(
        [gate_a.reshape(peer_count, chunk), gate_b.reshape(peer_count, rest)], axis=1
    )
    gates = jnp.pad(gates, ((0, 0), (0, model_width - capacity)))
    back_b = jnp.concatenate(
        [
            back_b.reshape(peer_count, rest, model_width),
            gates[:, None, :],
            jnp.zeros((peer_count, tail - rest - 1, model_width), back_b.dtype),
        ],
        axis=1,
    )
    returned_b = lax.all_to_all(back_b, "expert", 0, 0, tiled=True)
    gate_table = returned_b[:, rest, :capacity].reshape(-1)
    returned_b = returned_b.reshape(peer_count * tail, model_width)

    def weighted(weights, returned):
        return jnp.dot(
            weights,
            returned.astype(jnp.float32),
            precision=lax.Precision.HIGHEST,
            preferred_element_type=jnp.float32,
        )

    combined = grad_tokens.astype(jnp.float32) + weighted(weights_a, returned_a)
    combined = combined + jnp.dot(
        weights_b,
        returned_b.astype(jnp.float32),
        precision=lax.Precision.HIGH,
        preferred_element_type=jnp.float32,
    )
    gate_index = ids * capacity + places
    gate_hits = gate_index[:, :, None] == jnp.arange(gate_table.shape[0], dtype=jnp.int32)
    gate_slot = jnp.sum(
        jnp.where(gate_hits, gate_table.astype(jnp.float32), 0.0), axis=2
    ).astype(jnp.bfloat16)
    passed = passed_along(combined.astype(jnp.bfloat16)[None], "pipe", -1)
    return (passed, gate_slot[None])


def solution(mesh):
    placed = (
        P("pipe", "expert", None),
        P("pipe", "expert", None),
        P("pipe", "expert", None),
        P("pipe", "expert", None),
        P("pipe", "expert", None, None),
        P("pipe", "expert", None, None),
        P("pipe", "expert", None, None),
    )
    return jax.shard_map(
        body,
        mesh=mesh,
        in_specs=placed,
        out_specs=(P("pipe", "expert", None), P("pipe", "expert", None)),
        check_vma=False,
    )
```

```python
import jax
import jax.numpy as jnp
from jax import lax
from jax.experimental import pallas as pl
from jax.sharding import PartitionSpec as P


def passed_along(value, axis, steps):
    count = lax.axis_size(axis)
    first, last = (max(0, -steps), min(count, count - steps))
    return lax.ppermute(value, axis, [(source, source + steps) for source in range(first, last)])


def expert_rows(grad_rows, input_rows, gate_matrix, up_matrix, down_matrix):
    gate_pre = jnp.dot(input_rows, gate_matrix, preferred_element_type=jnp.float32)
    up_pre = jnp.dot(input_rows, up_matrix, preferred_element_type=jnp.float32)
    hidden_grad = lax.dot_general(
        grad_rows, down_matrix, (((1,), (1,)), ((), ())), preferred_element_type=jnp.float32
    )
    sigmoid = jax.nn.sigmoid(gate_pre)
    active = gate_pre * sigmoid
    gate_value = jnp.sum(hidden_grad * active * up_pre, axis=-1).astype(jnp.bfloat16)
    gate_part = (hidden_grad * up_pre * sigmoid * (1.0 + gate_pre * (1.0 - sigmoid))).astype(
        jnp.bfloat16
    )
    up_part = (hidden_grad * active).astype(jnp.bfloat16)
    input_back = lax.dot_general(
        gate_part, gate_matrix, (((1,), (1,)), ((), ())), preferred_element_type=jnp.float32
    ) + lax.dot_general(
        up_part, up_matrix, (((1,), (1,)), ((), ())), preferred_element_type=jnp.float32
    )
    return input_back.astype(jnp.bfloat16), gate_value


def expert_kernel(grad_ref, input_ref, gate_ref, up_ref, down_ref, back_ref, value_ref):
    grad_rows = grad_ref[...]
    input_rows = input_ref[...]
    gate_matrix = gate_ref[...]
    up_matrix = up_ref[...]
    gate_pre = jnp.dot(input_rows, gate_matrix, preferred_element_type=jnp.float32)
    up_pre = jnp.dot(input_rows, up_matrix, preferred_element_type=jnp.float32)
    hidden_grad = lax.dot_general(
        grad_rows, down_ref[...], (((1,), (1,)), ((), ())), preferred_element_type=jnp.float32
    )
    sigmoid = jax.nn.sigmoid(gate_pre)
    active = gate_pre * sigmoid
    value = jnp.sum(hidden_grad * active * up_pre, axis=-1, keepdims=True)
    value_ref[...] = jnp.broadcast_to(value, value_ref.shape)
    gate_part = (hidden_grad * up_pre * sigmoid * (1.0 + gate_pre * (1.0 - sigmoid))).astype(jnp.bfloat16)
    up_part = (hidden_grad * active).astype(jnp.bfloat16)
    back = lax.dot_general(
        gate_part, gate_matrix, (((1,), (1,)), ((), ())), preferred_element_type=jnp.float32
    ) + lax.dot_general(up_part, up_matrix, (((1,), (1,)), ((), ())), preferred_element_type=jnp.float32)
    back_ref[...] = back.astype(back_ref.dtype)

def expert_call(arrived, gate_matrix, up_matrix, down_matrix, tile=256):
    rows, both = arrived.shape
    width = both // 2
    hidden = gate_matrix.shape[1]
    steps = rows // tile
    flops = 2 * rows * width * hidden * 5
    cost = pl.CostEstimate(flops=flops, transcendentals=rows * hidden,
                           bytes_accessed=rows * both * 2 + 3 * width * hidden * 2 + rows * width * 2)
    back, value = pl.pallas_call(
        expert_kernel,
        grid=(steps,),
        in_specs=[
            pl.BlockSpec((tile, width), lambda i: (i, 0)),
            pl.BlockSpec((tile, width), lambda i: (i, 1)),
            pl.BlockSpec((width, hidden), lambda i: (0, 0)),
            pl.BlockSpec((width, hidden), lambda i: (0, 0)),
            pl.BlockSpec((hidden, width), lambda i: (0, 0)),
        ],
        out_specs=[
            pl.BlockSpec((tile, width), lambda i: (i, 0)),
            pl.BlockSpec((tile, 128), lambda i: (i, 0)),
        ],
        out_shape=[
            jax.ShapeDtypeStruct((rows, width), jnp.bfloat16),
            jax.ShapeDtypeStruct((rows, 128), jnp.float32),
        ],
        cost_estimate=cost,
    )(arrived, arrived, gate_matrix, up_matrix, down_matrix)
    return back, value[:, 0].astype(jnp.bfloat16)


def body(out_grad, layer_input, route_ids, route_probs, gate_weight, up_weight, down_weight):
    grad_tokens = out_grad[0]
    input_tokens = layer_input[0]
    chosen = route_ids[0]
    slot_probs = route_probs[0]
    gate_matrix = gate_weight[0, 0]
    up_matrix = up_weight[0, 0]
    down_matrix = down_weight[0, 0]
    peer_count = lax.axis_size("expert")
    token_count, top_count = chosen.shape
    model_width = grad_tokens.shape[1]
    capacity = min(token_count, 7 * token_count * top_count // (6 * peer_count))
    chunk = -(-(capacity + 1) // 16) * 8
    rows = peer_count * chunk

    named = chosen[:, :, None] == jnp.arange(peer_count, dtype=jnp.int32)[None, None, :]
    incidence = jnp.any(named, axis=1).astype(jnp.bfloat16)
    token_iota = jnp.arange(token_count, dtype=jnp.int32)
    earlier = (token_iota[None, :] < token_iota[:, None]).astype(jnp.bfloat16)
    before = jnp.dot(earlier, incidence, preferred_element_type=jnp.float32)
    places = jnp.sum(jnp.where(named, before[:, None, :], 0.0), axis=2).astype(jnp.int32)
    ids = chosen
    lanes = jnp.arange(rows, dtype=jnp.int32)[None, None, :]
    both = jnp.concatenate([grad_tokens, input_tokens], axis=1)

    def dispatch(part):
        local = places - part * chunk
        inside = (local >= 0) & (local < chunk)
        target = jnp.where(inside, ids * chunk + local, -1)
        hits = target[:, :, None] == lanes
        pick = jnp.any(target[None, :, :] == lanes.reshape(rows, 1, 1), axis=2)
        weights = jnp.sum(jnp.where(hits, slot_probs[:, :, None], 0.0), axis=1)
        return pick, weights

    pick_a, weights_a = dispatch(0)
    send_a = jnp.dot(pick_a.astype(jnp.bfloat16), both, preferred_element_type=jnp.bfloat16)
    send_a = send_a.reshape(peer_count, chunk, 2 * model_width)
    unused, weights_b = dispatch(1)
    rest = capacity - chunk
    local = places - chunk
    grad_row = jnp.where(local >= 0, ids * 2 * rest + local, -1)
    input_row = jnp.where(local >= 0, grad_row + rest, -1)
    send_lanes = jnp.arange(peer_count * 2 * rest, dtype=jnp.int32).reshape(-1, 1, 1)
    pick_grad = jnp.any(grad_row[None, :, :] == send_lanes, axis=2).astype(jnp.bfloat16)
    pick_input = jnp.any(input_row[None, :, :] == send_lanes, axis=2).astype(jnp.bfloat16)
    send_b = jnp.dot(pick_grad, grad_tokens, preferred_element_type=jnp.float32) + jnp.dot(
        pick_input, input_tokens, preferred_element_type=jnp.float32
    )
    send_b = send_b.astype(jnp.bfloat16).reshape(peer_count, 2 * rest, model_width)

    arrived_a = lax.all_to_all(send_a, "expert", 0, 0, tiled=True).reshape(rows, 2 * model_width)
    arrived_b = lax.all_to_all(send_b, "expert", 0, 0, tiled=True)
    back_a, gate_a = expert_call(arrived_a, gate_matrix, up_matrix, down_matrix)
    back_a, gate_a, arrived_b = lax.optimization_barrier((back_a, gate_a, arrived_b))
    returned_a = lax.all_to_all(
        back_a.reshape(peer_count, chunk, model_width), "expert", 0, 0, tiled=True
    ).reshape(rows, model_width)
    arrived_b = (
        arrived_b.reshape(peer_count, 2, rest, model_width)
        .transpose(0, 2, 1, 3)
        .reshape(peer_count * rest, 2 * model_width)
    )
    back_b, gate_b = expert_call(arrived_b, gate_matrix, up_matrix, down_matrix, tile=192)
    gates = jnp.concatenate(
        [gate_a.reshape(peer_count, chunk), gate_b.reshape(peer_count, rest)], axis=1
    )
    gates = jnp.pad(gates, ((0, 0), (0, model_width - capacity)))
    back_b = jnp.concatenate(
        [
            back_b.reshape(peer_count, rest, model_width),
            gates[:, None, :],
            jnp.zeros((peer_count, chunk - rest - 1, model_width), back_b.dtype),
        ],
        axis=1,
    )
    returned_b = lax.all_to_all(back_b, "expert", 0, 0, tiled=True)
    gate_table = returned_b[:, rest, :capacity].reshape(-1)
    returned_b = returned_b.reshape(rows, model_width)

    def weighted(weights, returned):
        return jnp.dot(
            weights,
            returned.astype(jnp.float32),
            precision=lax.Precision.HIGHEST,
            preferred_element_type=jnp.float32,
        )

    combined = grad_tokens.astype(jnp.float32) + weighted(weights_a, returned_a)
    combined = combined + jnp.dot(
        weights_b,
        returned_b.astype(jnp.float32),
        precision=lax.Precision.HIGH,
        preferred_element_type=jnp.float32,
    )
    gate_index = ids * capacity + places
    gate_hits = gate_index[:, :, None] == jnp.arange(gate_table.shape[0], dtype=jnp.int32)
    gate_slot = jnp.sum(
        jnp.where(gate_hits, gate_table.astype(jnp.float32), 0.0), axis=2
    ).astype(jnp.bfloat16)
    passed = passed_along(combined.astype(jnp.bfloat16)[None], "pipe", -1)
    return (passed, gate_slot[None])


def solution(mesh):
    placed = (
        P("pipe", "expert", None),
        P("pipe", "expert", None),
        P("pipe", "expert", None),
        P("pipe", "expert", None),
        P("pipe", "expert", None, None),
        P("pipe", "expert", None, None),
        P("pipe", "expert", None, None),
    )
    return jax.shard_map(
        body,
        mesh=mesh,
        in_specs=placed,
        out_specs=(P("pipe", "expert", None), P("pipe", "expert", None)),
        check_vma=False,
    )
```

```python
import jax
import jax.numpy as jnp
from jax import lax
from jax.experimental import pallas as pl
from jax.sharding import PartitionSpec as P


def passed_along(value, axis, steps):
    count = lax.axis_size(axis)
    first, last = (max(0, -steps), min(count, count - steps))
    return lax.ppermute(value, axis, [(source, source + steps) for source in range(first, last)])


def expert_rows(grad_rows, input_rows, gate_matrix, up_matrix, down_matrix):
    gate_pre = jnp.dot(input_rows, gate_matrix, preferred_element_type=jnp.float32)
    up_pre = jnp.dot(input_rows, up_matrix, preferred_element_type=jnp.float32)
    hidden_grad = lax.dot_general(
        grad_rows, down_matrix, (((1,), (1,)), ((), ())), preferred_element_type=jnp.float32
    )
    sigmoid = jax.nn.sigmoid(gate_pre)
    active = gate_pre * sigmoid
    gate_value = jnp.sum(hidden_grad * active * up_pre, axis=-1).astype(jnp.bfloat16)
    gate_part = (hidden_grad * up_pre * sigmoid * (1.0 + gate_pre * (1.0 - sigmoid))).astype(
        jnp.bfloat16
    )
    up_part = (hidden_grad * active).astype(jnp.bfloat16)
    input_back = lax.dot_general(
        gate_part, gate_matrix, (((1,), (1,)), ((), ())), preferred_element_type=jnp.float32
    ) + lax.dot_general(
        up_part, up_matrix, (((1,), (1,)), ((), ())), preferred_element_type=jnp.float32
    )
    return input_back.astype(jnp.bfloat16), gate_value


def expert_kernel(grad_ref, input_ref, gate_ref, up_ref, down_ref, back_ref, value_ref):
    grad_rows = grad_ref[...]
    input_rows = input_ref[...]
    gate_matrix = gate_ref[...]
    up_matrix = up_ref[...]
    gate_pre = jnp.dot(input_rows, gate_matrix, preferred_element_type=jnp.float32)
    up_pre = jnp.dot(input_rows, up_matrix, preferred_element_type=jnp.float32)
    hidden_grad = lax.dot_general(
        grad_rows, down_ref[...], (((1,), (1,)), ((), ())), preferred_element_type=jnp.float32
    )
    sigmoid = jax.nn.sigmoid(gate_pre)
    active = gate_pre * sigmoid
    value = jnp.sum(hidden_grad * active * up_pre, axis=-1, keepdims=True)
    value_ref[...] = jnp.broadcast_to(value, value_ref.shape)
    gate_part = (hidden_grad * up_pre * sigmoid * (1.0 + gate_pre * (1.0 - sigmoid))).astype(jnp.bfloat16)
    up_part = (hidden_grad * active).astype(jnp.bfloat16)
    back = lax.dot_general(
        gate_part, gate_matrix, (((1,), (1,)), ((), ())), preferred_element_type=jnp.float32
    ) + lax.dot_general(up_part, up_matrix, (((1,), (1,)), ((), ())), preferred_element_type=jnp.float32)
    back_ref[...] = back.astype(back_ref.dtype)

def expert_call(arrived, gate_matrix, up_matrix, down_matrix, tile=256):
    rows, both = arrived.shape
    width = both // 2
    hidden = gate_matrix.shape[1]
    steps = rows // tile
    flops = 2 * rows * width * hidden * 5
    cost = pl.CostEstimate(flops=flops, transcendentals=rows * hidden,
                           bytes_accessed=rows * both * 2 + 3 * width * hidden * 2 + rows * width * 2)
    back, value = pl.pallas_call(
        expert_kernel,
        grid=(steps,),
        in_specs=[
            pl.BlockSpec((tile, width), lambda i: (i, 0)),
            pl.BlockSpec((tile, width), lambda i: (i, 1)),
            pl.BlockSpec((width, hidden), lambda i: (0, 0)),
            pl.BlockSpec((width, hidden), lambda i: (0, 0)),
            pl.BlockSpec((hidden, width), lambda i: (0, 0)),
        ],
        out_specs=[
            pl.BlockSpec((tile, width), lambda i: (i, 0)),
            pl.BlockSpec((tile, 128), lambda i: (i, 0)),
        ],
        out_shape=[
            jax.ShapeDtypeStruct((rows, width), jnp.bfloat16),
            jax.ShapeDtypeStruct((rows, 128), jnp.float32),
        ],
        cost_estimate=cost,
    )(arrived, arrived, gate_matrix, up_matrix, down_matrix)
    return back, value[:, 0].astype(jnp.bfloat16)


def body(out_grad, layer_input, route_ids, route_probs, gate_weight, up_weight, down_weight):
    grad_tokens = out_grad[0]
    input_tokens = layer_input[0]
    chosen = route_ids[0]
    slot_probs = route_probs[0]
    gate_matrix = gate_weight[0, 0]
    up_matrix = up_weight[0, 0]
    down_matrix = down_weight[0, 0]
    peer_count = lax.axis_size("expert")
    token_count, top_count = chosen.shape
    model_width = grad_tokens.shape[1]
    capacity = min(token_count, 7 * token_count * top_count // (6 * peer_count))
    chunk = -(-(capacity + 1) // 16) * 8
    rows = peer_count * chunk

    named = chosen[:, :, None] == jnp.arange(peer_count, dtype=jnp.int32)[None, None, :]
    incidence = jnp.any(named, axis=1).astype(jnp.bfloat16)
    token_iota = jnp.arange(token_count, dtype=jnp.int32)
    earlier = (token_iota[None, :] < token_iota[:, None]).astype(jnp.bfloat16)
    before = jnp.dot(earlier, incidence, preferred_element_type=jnp.float32)
    places = jnp.sum(jnp.where(named, before[:, None, :], 0.0), axis=2).astype(jnp.int32)
    ids = chosen
    lanes = jnp.arange(rows, dtype=jnp.int32)[None, None, :]
    both = jnp.concatenate([grad_tokens, input_tokens], axis=1)

    def dispatch(part):
        local = places - part * chunk
        inside = (local >= 0) & (local < chunk)
        target = jnp.where(inside, ids * chunk + local, -1)
        hits = target[:, :, None] == lanes
        pick = jnp.any(target[None, :, :] == lanes.reshape(rows, 1, 1), axis=2)
        weights = jnp.sum(jnp.where(hits, slot_probs[:, :, None], 0.0), axis=1)
        return pick, weights

    pick_a, weights_a = dispatch(0)
    send_a = jnp.dot(pick_a.astype(jnp.bfloat16), both, preferred_element_type=jnp.float32)
    send_a = send_a.astype(jnp.bfloat16).reshape(peer_count, chunk, 2 * model_width)
    unused, weights_b = dispatch(1)
    rest = capacity - chunk
    local = places - chunk
    grad_row = jnp.where(local >= 0, ids * 2 * rest + local, -1)
    input_row = jnp.where(local >= 0, grad_row + rest, -1)
    send_lanes = jnp.arange(peer_count * 2 * rest, dtype=jnp.int32).reshape(-1, 1, 1)
    pick_grad = jnp.any(grad_row[None, :, :] == send_lanes, axis=2).astype(jnp.bfloat16)
    pick_input = jnp.any(input_row[None, :, :] == send_lanes, axis=2).astype(jnp.bfloat16)
    send_b = jnp.dot(pick_grad, grad_tokens, preferred_element_type=jnp.float32) + jnp.dot(
        pick_input, input_tokens, preferred_element_type=jnp.float32
    )
    send_b = send_b.astype(jnp.bfloat16).reshape(peer_count, 2 * rest, model_width)

    arrived_a = lax.all_to_all(send_a, "expert", 0, 0, tiled=True).reshape(rows, 2 * model_width)
    arrived_b = lax.all_to_all(send_b, "expert", 0, 0, tiled=True)
    back_a, gate_a = expert_call(arrived_a, gate_matrix, up_matrix, down_matrix)
    back_a, gate_a, arrived_b = lax.optimization_barrier((back_a, gate_a, arrived_b))
    returned_a = lax.all_to_all(
        back_a.reshape(peer_count, chunk, model_width), "expert", 0, 0, tiled=True
    ).reshape(rows, model_width)
    arrived_b = (
        arrived_b.reshape(peer_count, 2, rest, model_width)
        .transpose(0, 2, 1, 3)
        .reshape(peer_count * rest, 2 * model_width)
    )
    back_b, gate_b = expert_call(arrived_b, gate_matrix, up_matrix, down_matrix, tile=384)
    gates = jnp.concatenate(
        [gate_a.reshape(peer_count, chunk), gate_b.reshape(peer_count, rest)], axis=1
    )
    gates = jnp.pad(gates, ((0, 0), (0, model_width - capacity)))
    back_b = jnp.concatenate(
        [
            back_b.reshape(peer_count, rest, model_width),
            gates[:, None, :],
            jnp.zeros((peer_count, chunk - rest - 1, model_width), back_b.dtype),
        ],
        axis=1,
    )
    returned_b = lax.all_to_all(back_b, "expert", 0, 0, tiled=True)
    gate_table = returned_b[:, rest, :capacity].reshape(-1)
    returned_b = returned_b.reshape(rows, model_width)

    def weighted(weights, returned):
        return jnp.dot(
            weights,
            returned.astype(jnp.float32),
            precision=lax.Precision.HIGHEST,
            preferred_element_type=jnp.float32,
        )

    combined = grad_tokens.astype(jnp.float32) + weighted(weights_a, returned_a)
    combined = combined + jnp.dot(
        weights_b,
        returned_b.astype(jnp.float32),
        precision=lax.Precision.HIGH,
        preferred_element_type=jnp.float32,
    )
    gate_index = ids * capacity + places
    gate_hits = gate_index[:, :, None] == jnp.arange(gate_table.shape[0], dtype=jnp.int32)
    gate_slot = jnp.sum(
        jnp.where(gate_hits, gate_table.astype(jnp.float32), 0.0), axis=2
    ).astype(jnp.bfloat16)
    passed = passed_along(combined.astype(jnp.bfloat16)[None], "pipe", -1)
    return (passed, gate_slot[None])


def solution(mesh):
    placed = (
        P("pipe", "expert", None),
        P("pipe", "expert", None),
        P("pipe", "expert", None),
        P("pipe", "expert", None),
        P("pipe", "expert", None, None),
        P("pipe", "expert", None, None),
        P("pipe", "expert", None, None),
    )
    return jax.shard_map(
        body,
        mesh=mesh,
        in_specs=placed,
        out_specs=(P("pipe", "expert", None), P("pipe", "expert", None)),
        check_vma=False,
    )
```

```python
import jax
import jax.numpy as jnp
from jax import lax
from jax.experimental import pallas as pl
from jax.sharding import PartitionSpec as P


def passed_along(value, axis, steps):
    count = lax.axis_size(axis)
    first, last = (max(0, -steps), min(count, count - steps))
    return lax.ppermute(value, axis, [(source, source + steps) for source in range(first, last)])


def expert_rows(grad_rows, input_rows, gate_matrix, up_matrix, down_matrix):
    gate_pre = jnp.dot(input_rows, gate_matrix, preferred_element_type=jnp.float32)
    up_pre = jnp.dot(input_rows, up_matrix, preferred_element_type=jnp.float32)
    hidden_grad = lax.dot_general(
        grad_rows, down_matrix, (((1,), (1,)), ((), ())), preferred_element_type=jnp.float32
    )
    sigmoid = jax.nn.sigmoid(gate_pre)
    active = gate_pre * sigmoid
    gate_value = jnp.sum(hidden_grad * active * up_pre, axis=-1).astype(jnp.bfloat16)
    gate_part = (hidden_grad * up_pre * sigmoid * (1.0 + gate_pre * (1.0 - sigmoid))).astype(
        jnp.bfloat16
    )
    up_part = (hidden_grad * active).astype(jnp.bfloat16)
    input_back = lax.dot_general(
        gate_part, gate_matrix, (((1,), (1,)), ((), ())), preferred_element_type=jnp.float32
    ) + lax.dot_general(
        up_part, up_matrix, (((1,), (1,)), ((), ())), preferred_element_type=jnp.float32
    )
    return input_back.astype(jnp.bfloat16), gate_value


def expert_kernel(grad_ref, input_ref, gate_ref, up_ref, down_ref, back_ref, value_ref):
    grad_rows = grad_ref[...]
    input_rows = input_ref[...]
    gate_matrix = gate_ref[...]
    up_matrix = up_ref[...]
    gate_pre = jnp.dot(input_rows, gate_matrix, preferred_element_type=jnp.float32)
    up_pre = jnp.dot(input_rows, up_matrix, preferred_element_type=jnp.float32)
    hidden_grad = lax.dot_general(
        grad_rows, down_ref[...], (((1,), (1,)), ((), ())), preferred_element_type=jnp.float32
    )
    sigmoid = jax.nn.sigmoid(gate_pre)
    active = gate_pre * sigmoid
    value = jnp.sum(hidden_grad * active * up_pre, axis=-1, keepdims=True)
    value_ref[...] = jnp.broadcast_to(value, value_ref.shape)
    gate_part = (hidden_grad * up_pre * sigmoid * (1.0 + gate_pre * (1.0 - sigmoid))).astype(jnp.bfloat16)
    up_part = (hidden_grad * active).astype(jnp.bfloat16)
    back = lax.dot_general(
        gate_part, gate_matrix, (((1,), (1,)), ((), ())), preferred_element_type=jnp.float32
    ) + lax.dot_general(up_part, up_matrix, (((1,), (1,)), ((), ())), preferred_element_type=jnp.float32)
    back_ref[...] = back.astype(back_ref.dtype)

def expert_call(arrived, gate_matrix, up_matrix, down_matrix, tile=256):
    rows, both = arrived.shape
    width = both // 2
    hidden = gate_matrix.shape[1]
    steps = rows // tile
    flops = 2 * rows * width * hidden * 5
    cost = pl.CostEstimate(flops=flops, transcendentals=rows * hidden,
                           bytes_accessed=rows * both * 2 + 3 * width * hidden * 2 + rows * width * 2)
    back, value = pl.pallas_call(
        expert_kernel,
        grid=(steps,),
        in_specs=[
            pl.BlockSpec((tile, width), lambda i: (i, 0)),
            pl.BlockSpec((tile, width), lambda i: (i, 1)),
            pl.BlockSpec((width, hidden), lambda i: (0, 0)),
            pl.BlockSpec((width, hidden), lambda i: (0, 0)),
            pl.BlockSpec((hidden, width), lambda i: (0, 0)),
        ],
        out_specs=[
            pl.BlockSpec((tile, width), lambda i: (i, 0)),
            pl.BlockSpec((tile, 128), lambda i: (i, 0)),
        ],
        out_shape=[
            jax.ShapeDtypeStruct((rows, width), jnp.bfloat16),
            jax.ShapeDtypeStruct((rows, 128), jnp.float32),
        ],
        cost_estimate=cost,
    )(arrived, arrived, gate_matrix, up_matrix, down_matrix)
    return back, value[:, 0].astype(jnp.bfloat16)


def body(out_grad, layer_input, route_ids, route_probs, gate_weight, up_weight, down_weight):
    grad_tokens = out_grad[0]
    input_tokens = layer_input[0]
    chosen = route_ids[0]
    slot_probs = route_probs[0]
    gate_matrix = gate_weight[0, 0]
    up_matrix = up_weight[0, 0]
    down_matrix = down_weight[0, 0]
    peer_count = lax.axis_size("expert")
    token_count, top_count = chosen.shape
    model_width = grad_tokens.shape[1]
    capacity = min(token_count, 7 * token_count * top_count // (6 * peer_count))
    chunk = -(-(capacity + 1) // 16) * 8
    rows = peer_count * chunk

    named = chosen[:, :, None] == jnp.arange(peer_count, dtype=jnp.int32)[None, None, :]
    incidence = jnp.any(named, axis=1).astype(jnp.bfloat16)
    token_iota = jnp.arange(token_count, dtype=jnp.int32)
    earlier = (token_iota[None, :] < token_iota[:, None]).astype(jnp.bfloat16)
    before = jnp.dot(earlier, incidence, preferred_element_type=jnp.float32)
    places = jnp.sum(jnp.where(named, before[:, None, :], 0.0), axis=2).astype(jnp.int32)
    ids = chosen
    lanes = jnp.arange(rows, dtype=jnp.int32)[None, None, :]
    both = jnp.concatenate([grad_tokens, input_tokens], axis=1)

    def dispatch(part):
        local = places - part * chunk
        inside = (local >= 0) & (local < chunk)
        target = jnp.where(inside, ids * chunk + local, -1)
        hits = target[:, :, None] == lanes
        pick = jnp.any(target[None, :, :] == lanes.reshape(rows, 1, 1), axis=2)
        weights = jnp.sum(jnp.where(hits, slot_probs[:, :, None], 0.0), axis=1)
        return pick, weights

    pick_a, weights_a = dispatch(0)
    send_a = jnp.dot(pick_a.astype(jnp.bfloat16), both, preferred_element_type=jnp.float32)
    send_a = send_a.astype(jnp.bfloat16).reshape(peer_count, chunk, 2 * model_width)
    unused, weights_b = dispatch(1)
    rest = capacity - chunk
    local = places - chunk
    grad_row = jnp.where(local >= 0, ids * 2 * rest + local, -1)
    input_row = jnp.where(local >= 0, grad_row + rest, -1)
    send_lanes = jnp.arange(peer_count * 2 * rest, dtype=jnp.int32).reshape(-1, 1, 1)
    pick_grad = jnp.any(grad_row[None, :, :] == send_lanes, axis=2).astype(jnp.bfloat16)
    pick_input = jnp.any(input_row[None, :, :] == send_lanes, axis=2).astype(jnp.bfloat16)
    send_b = jnp.dot(pick_grad, grad_tokens, preferred_element_type=jnp.float32) + jnp.dot(
        pick_input, input_tokens, preferred_element_type=jnp.float32
    )
    send_b = send_b.astype(jnp.bfloat16).reshape(peer_count, 2 * rest, model_width)

    arrived_a = lax.all_to_all(send_a, "expert", 0, 0, tiled=True).reshape(rows, 2 * model_width)
    arrived_b = lax.all_to_all(send_b, "expert", 0, 0, tiled=True)
    back_a, gate_a = expert_call(arrived_a, gate_matrix, up_matrix, down_matrix)
    back_a, gate_a, arrived_b = lax.optimization_barrier((back_a, gate_a, arrived_b))
    returned_a = lax.all_to_all(
        back_a.reshape(peer_count, chunk, model_width), "expert", 0, 0, tiled=True
    ).reshape(rows, model_width)
    arrived_b = jnp.concatenate([arrived_b[:, :rest], arrived_b[:, rest:]], axis=2).reshape(
        peer_count * rest, 2 * model_width
    )
    back_b, gate_b = expert_call(arrived_b, gate_matrix, up_matrix, down_matrix, tile=384)
    gates = jnp.concatenate(
        [gate_a.reshape(peer_count, chunk), gate_b.reshape(peer_count, rest)], axis=1
    )
    gates = jnp.pad(gates, ((0, 0), (0, model_width - capacity)))
    back_b = jnp.concatenate(
        [
            back_b.reshape(peer_count, rest, model_width),
            gates[:, None, :],
            jnp.zeros((peer_count, chunk - rest - 1, model_width), back_b.dtype),
        ],
        axis=1,
    )
    returned_b = lax.all_to_all(back_b, "expert", 0, 0, tiled=True)
    gate_table = returned_b[:, rest, :capacity].reshape(-1)
    returned_b = returned_b.reshape(rows, model_width)

    def weighted(weights, returned):
        return jnp.dot(
            weights,
            returned.astype(jnp.float32),
            precision=lax.Precision.HIGHEST,
            preferred_element_type=jnp.float32,
        )

    combined = grad_tokens.astype(jnp.float32) + weighted(weights_a, returned_a)
    combined = combined + jnp.dot(
        weights_b,
        returned_b.astype(jnp.float32),
        precision=lax.Precision.HIGH,
        preferred_element_type=jnp.float32,
    )
    gate_index = ids * capacity + places
    gate_hits = gate_index[:, :, None] == jnp.arange(gate_table.shape[0], dtype=jnp.int32)
    gate_slot = jnp.sum(
        jnp.where(gate_hits, gate_table.astype(jnp.float32), 0.0), axis=2
    ).astype(jnp.bfloat16)
    passed = passed_along(combined.astype(jnp.bfloat16)[None], "pipe", -1)
    return (passed, gate_slot[None])


def solution(mesh):
    placed = (
        P("pipe", "expert", None),
        P("pipe", "expert", None),
        P("pipe", "expert", None),
        P("pipe", "expert", None),
        P("pipe", "expert", None, None),
        P("pipe", "expert", None, None),
        P("pipe", "expert", None, None),
    )
    return jax.shard_map(
        body,
        mesh=mesh,
        in_specs=placed,
        out_specs=(P("pipe", "expert", None), P("pipe", "expert", None)),
        check_vma=False,
    )
```
